32 devices in a mesh: row: 16 (over z, x, core), col: 2 (over y).
Axes of the slice: x: 2, y: 2, z: 4, core: 2. Of those that a mesh axis runs over, the one named last changes fastest.
Arguments:
- slab: float32 [8192, 1024], P('row', 'col'), may hold values from -6 to 6
- leaf_v: float32 [8192, 256], P('row', 'col'), may hold values from -0.25 to 0.25
- leaf_t: float32 [4096, 256], P('row', 'col'), may hold values from -0.1875 to 0.1875
- tree_v: float32 [4096, 256], P('row', 'col'), may hold values from -0.375 to 0.375
- tree_t: float32 [4096, 256], P('row', 'col'), may hold values from -0.1875 to 0.1875
Outputs:
- updated_slab: float32 [8192, 1024], P('row', 'col')
The draws below stay inside these ranges and needn't reach their ends.
All inputs are finite; a program needn't handle non-finite values.
Results may differ from the reference program's by a relative error of at most 0.0001.
Values sent between devices are 32-bit elements; how exact they have to be, the bound alone decides.
No kernel may reach another device: no remote copies, remote signals or barrier semaphores. Data moves between devices by JAX's collectives and lax.ppermute only.
A program may use at most 64 MiB of HBM per device.

```python
import jax
import jax.numpy as jnp
from jax import lax

B = 256
ROWS_DEV = 512
ROWS = 8192
COLS = 1024
SECTIONS = 4
N_ROW = 16


def steps_of(rng, dims, split, low, top_value):
    def one(position, parts):
        steps = jax.random.uniform(jax.random.fold_in(jax.random.fold_in(rng, 6), position), (parts,), jnp.float32, low / len(split), top_value / len(split))
        return jnp.repeat(jnp.exp(steps), dims[position] // parts).reshape((-1,) + (1,) * (len(dims) - position - 1))

    level = one(*split[0])
    for cut in split[1:]:
        level = level * one(*cut)
    return level


def bell_draw(stream_key, dims, scale, bound, cuts=(), kind=jnp.bfloat16):
    loudness = steps_of(stream_key, dims, cuts, -0.22, 0.18) if cuts else 1.0
    values = jax.random.normal(stream_key, dims, jnp.float32) * scale * loudness
    return jnp.minimum(jnp.maximum(values, -bound), bound).astype(kind)


def setup_inputs(seed: int = 0) -> dict:
    splits = jax.random.split(jax.random.key(seed), 6)
    slab = bell_draw(splits[0], (ROWS, COLS), 1.0, 6.0, ((0, 16), (1, 2)), jnp.float32)
    leaf_v = bell_draw(splits[1], (ROWS, B), ROWS_DEV ** -0.5, 0.25, ((0, 16), (1, 2)), jnp.float32)
    leaf_t = bell_draw(splits[2], (N_ROW * B, B), (4 * B) ** -0.5, 0.1875, ((0, 16), (1, 2)), jnp.float32)
    tree_v = bell_draw(splits[3], (N_ROW * B, B), B ** -0.5, 0.375, ((0, 16), (1, 2)), jnp.float32)
    tree_t = bell_draw(splits[4], (N_ROW * B, B), (4 * B) ** -0.5, 0.1875, ((0, 16), (1, 2)), jnp.float32)
    return dict(slab=slab, leaf_v=leaf_v, leaf_t=leaf_t, tree_v=tree_v, tree_t=tree_t)


def reference(slab, leaf_v, leaf_t, tree_v, tree_t):
    highest = lax.Precision.HIGHEST
    row_ids = lax.broadcasted_iota(jnp.int32, (ROWS_DEV, B), 0)
    col_ids = lax.broadcasted_iota(jnp.int32, (ROWS_DEV, B), 1)
    blocks = slab.reshape(N_ROW, ROWS_DEV, COLS)
    diagonal = jnp.where(row_ids == col_ids, 1.0, 0.0).astype(slab.dtype)
    vectors = jnp.where(row_ids > col_ids, leaf_v.reshape(N_ROW, ROWS_DEV, B), 0.0) + diagonal
    leaf_factor = jnp.triu(leaf_t.reshape(N_ROW, B, B))
    tree_vectors = jnp.triu(tree_v.reshape(N_ROW, B, B))
    tree_factor = jnp.triu(tree_t.reshape(N_ROW, B, B))
    inner = jnp.einsum("nrk,nrc->nkc", vectors, blocks, precision=highest)
    leaf_w = jnp.einsum("nrk,nrc->nkc", leaf_factor, inner, precision=highest)
    blocks = blocks - jnp.einsum("nrk,nkc->nrc", vectors, leaf_w, precision=highest)
    tops = blocks[:, :B, :]
    for level in range(SECTIONS):
        step = 2 ** level
        lower_rows = tops[0::2 * step]
        upper_rows = tops[step::2 * step]
        pair_vectors = tree_vectors[step::2 * step]
        pair_factor = tree_factor[step::2 * step]
        merged = lower_rows + jnp.einsum("nrk,nrc->nkc", pair_vectors, upper_rows, precision=highest)
        update = jnp.einsum("nrk,nrc->nkc", pair_factor, merged, precision=highest)
        raised = upper_rows - jnp.einsum("nrk,nkc->nrc", pair_vectors, update, precision=highest)
        tops = tops.at[0::2 * step].set(lower_rows - update)
        tops = tops.at[step::2 * step].set(raised)
    result = jnp.concatenate([tops, blocks[:, B:, :]], axis=1)
    return result.reshape(ROWS, COLS)
```

```python
import jax
import jax.numpy as jnp
from jax import lax
from jax.sharding import PartitionSpec as P


def product(left, right):
    return jnp.dot(left, right, precision=lax.Precision.HIGHEST, preferred_element_type=jnp.float32)


def product_left_t(left, right):
    return lax.dot_general(
        left,
        right,
        (((0,), (0,)), ((), ())),
        precision=lax.Precision.HIGHEST,
        preferred_element_type=jnp.float32,
    )


def unit_lower(raw):
    row_ids = lax.broadcasted_iota(jnp.int32, raw.shape, 0)
    col_ids = lax.broadcasted_iota(jnp.int32, raw.shape, 1)
    diagonal = jnp.where(row_ids == col_ids, 1.0, 0.0).astype(raw.dtype)
    return jnp.where(row_ids > col_ids, raw, 0.0) + diagonal


def col_gather(parts):
    n_col = lax.axis_size("col")
    me = lax.axis_index("col")
    by_shift = [parts]
    for shift in range(1, n_col):
        perm = [(i, (i + shift) % n_col) for i in range(n_col)]
        by_shift.append(lax.ppermute(parts, "col", perm))
    joined = []
    for a in range(len(parts)):
        stacked = jnp.stack([got[a] for got in by_shift])
        blocks = [stacked[(me - b) % n_col] for b in range(n_col)]
        joined.append(jnp.concatenate(blocks, axis=1))
    return joined


def on_device(slab, leaf_v, leaf_t, tree_v, tree_t):
    n_row = lax.axis_size("row")
    levels = n_row.bit_length() - 1
    position = lax.axis_index("row")

    leaf_full, leaf_tri = col_gather((leaf_v, leaf_t))
    tree_full, tree_tri = col_gather((tree_v, tree_t))
    width = leaf_tri.shape[0]

    leaf_vectors = unit_lower(leaf_full)
    leaf_factor = jnp.triu(leaf_tri)
    leaf_w = product_left_t(leaf_factor, product_left_t(leaf_vectors, slab))
    current = slab[:width] - product(leaf_vectors[:width], leaf_w)
    remainder = slab[width:] - product(leaf_vectors[width:], leaf_w)

    tree_vectors = jnp.triu(tree_full)
    tree_factor = jnp.triu(tree_tri)
    tree_joint = product(tree_vectors, tree_factor)

    partner_factors = []
    for level in range(levels):
        step = 1 << level
        pairs = [(i + step, i) for i in range(0, n_row, 2 * step)]
        partner_factors.append(lax.ppermute((tree_factor, tree_joint), "row", pairs))

    for level in range(levels):
        if level < 2:
            wanted = partner_factors[0] if level == 0 else partner_factors[1:]
            current, wanted = lax.optimization_barrier((current, wanted))
            if level == 0:
                partner_factors[0] = wanted
            else:
                partner_factors[1:] = wanted
        step = 1 << level
        phase = position % (2 * step)
        role = jnp.where(phase == 0, 1, jnp.where(phase == step, 2, 0))
        pairs = []
        for i in range(0, n_row, 2 * step):
            pairs += [(i, i + step), (i + step, i)]
        received = lax.ppermute(current, "row", pairs)
        their_factor, their_joint = partner_factors[level]

        def idle_pre(g, sf):
            return g

        def lower_pre(g, sf):
            return g - product_left_t(sf, g)

        def upper_pre(g, sf):
            return product_left_t(tree_joint, g)

        early = lax.switch(role, (idle_pre, lower_pre, upper_pre), current, their_factor)

        def idle_post(g, e, r, sj):
            return g

        def lower_post(g, e, r, sj):
            return e - product_left_t(sj, r)

        def upper_post(g, e, r, sj):
            return g - product(tree_vectors, product_left_t(tree_factor, r) + e)

        current = lax.switch(role, (idle_post, lower_post, upper_post), current, early, received, their_joint)
    return jnp.concatenate([current, remainder], axis=0)


def solution(mesh):
    in_specs = (P("row", "col"), P("row", "col"), P("row", "col"), P("row", "col"), P("row", "col"))
    out_specs = P("row", "col")
    return jax.shard_map(
        on_device, mesh=mesh, in_specs=in_specs, out_specs=out_specs, check_vma=False
    )
```

```python
import jax
import jax.numpy as jnp
from jax import lax
from jax.sharding import PartitionSpec as P


def product(left, right):
    return jnp.dot(left, right, precision=lax.Precision.HIGHEST, preferred_element_type=jnp.float32)


def product_left_t(left, right):
    return lax.dot_general(
        left,
        right,
        (((0,), (0,)), ((), ())),
        precision=lax.Precision.HIGHEST,
        preferred_element_type=jnp.float32,
    )


def unit_lower(raw):
    row_ids = lax.broadcasted_iota(jnp.int32, raw.shape, 0)
    col_ids = lax.broadcasted_iota(jnp.int32, raw.shape, 1)
    diagonal = jnp.where(row_ids == col_ids, 1.0, 0.0).astype(raw.dtype)
    return jnp.where(row_ids > col_ids, raw, 0.0) + diagonal


def col_gather(part):
    n_col = lax.axis_size("col")
    me = lax.axis_index("col")
    by_shift = [part]
    for shift in range(1, n_col):
        perm = [(i, (i + shift) % n_col) for i in range(n_col)]
        by_shift.append(lax.ppermute(part, "col", perm))
    stacked = jnp.stack(by_shift)
    blocks = [stacked[(me - b) % n_col] for b in range(n_col)]
    return jnp.concatenate(blocks, axis=1)


def on_device(slab, leaf_v, leaf_t, tree_v, tree_t):
    n_row = lax.axis_size("row")
    levels = n_row.bit_length() - 1
    position = lax.axis_index("row")
    rows = leaf_v.shape[0]
    width = leaf_t.shape[0]

    gathered = col_gather(jnp.concatenate([leaf_v, leaf_t, tree_v, tree_t], axis=0))
    leaf_full = gathered[:rows]
    leaf_tri = gathered[rows:rows + width]
    tree_full = gathered[rows + width:rows + 2 * width]
    tree_tri = gathered[rows + 2 * width:]

    leaf_vectors = unit_lower(leaf_full)
    leaf_factor = jnp.triu(leaf_tri)
    leaf_w = product_left_t(leaf_factor, product_left_t(leaf_vectors, slab))
    leafed = slab - product(leaf_vectors, leaf_w)
    current = leafed[:width]

    tree_vectors = jnp.triu(tree_full)
    tree_factor = jnp.triu(tree_tri)
    tree_joint = product(tree_vectors, tree_factor)
    own_pair = jnp.stack([tree_factor, tree_joint])

    partner_factors = []
    for level in range(levels):
        step = 1 << level
        pairs = [(i + step, i) for i in range(0, n_row, 2 * step)]
        partner_factors.append(lax.ppermute(own_pair, "row", pairs))

    zeros = jnp.zeros_like(tree_factor)
    result = current
    for level in range(levels):
        if level < 2:
            wanted = partner_factors[0] if level == 0 else partner_factors[1:]
            current, wanted = lax.optimization_barrier((current, wanted))
            if level == 0:
                partner_factors[0] = wanted
            else:
                partner_factors[1:] = wanted
        step = 1 << level
        phase = position % (2 * step)
        is_lower = phase == 0
        is_upper = phase == step
        their = partner_factors[level]
        first = jnp.where(is_lower, their[0], jnp.where(is_upper, tree_joint, zeros))
        second = jnp.where(is_lower, their[1], jnp.where(is_upper, tree_factor, zeros))
        pairs = []
        for i in range(0, n_row, 2 * step):
            pairs += [(i, i + step), (i + step, i)]
        received = lax.ppermute(current, "row", pairs)
        early = product_left_t(first, current)
        early, received = lax.optimization_barrier((early, received))
        update = early + product_left_t(second, received)
        result = jnp.where(is_upper, current - product(tree_vectors, update), result)
        current = jnp.where(is_lower, current - update, current)
    top = jnp.where(position == 0, current, result)
    return lax.dynamic_update_slice(leafed, top, (0, 0))


def solution(mesh):
    in_specs = (P("row", "col"), P("row", "col"), P("row", "col"), P("row", "col"), P("row", "col"))
    out_specs = P("row", "col")
    return jax.shard_map(
        on_device, mesh=mesh, in_specs=in_specs, out_specs=out_specs, check_vma=False
    )
```

```python
import jax
import jax.numpy as jnp
from jax import lax
from jax.sharding import PartitionSpec as P


def product(left, right):
    return jnp.dot(left, right, precision=lax.Precision.HIGHEST, preferred_element_type=jnp.float32)


def product_left_t(left, right):
    return lax.dot_general(
        left,
        right,
        (((0,), (0,)), ((), ())),
        precision=lax.Precision.HIGHEST,
        preferred_element_type=jnp.float32,
    )


def unit_lower(raw):
    row_ids = lax.broadcasted_iota(jnp.int32, raw.shape, 0)
    col_ids = lax.broadcasted_iota(jnp.int32, raw.shape, 1)
    diagonal = jnp.where(row_ids == col_ids, 1.0, 0.0).astype(raw.dtype)
    return jnp.where(row_ids > col_ids, raw, 0.0) + diagonal


def col_gather(part):
    n_col = lax.axis_size("col")
    me = lax.axis_index("col")
    by_shift = [part]
    for shift in range(1, n_col):
        perm = [(i, (i + shift) % n_col) for i in range(n_col)]
        by_shift.append(lax.ppermute(part, "col", perm))
    stacked = jnp.stack(by_shift)
    blocks = [stacked[(me - b) % n_col] for b in range(n_col)]
    return jnp.concatenate(blocks, axis=1)


def on_device(slab, leaf_v, leaf_t, tree_v, tree_t):
    n_row = lax.axis_size("row")
    levels = n_row.bit_length() - 1
    position = lax.axis_index("row")
    rows = leaf_v.shape[0]
    width = leaf_t.shape[0]

    gathered = col_gather(jnp.concatenate([leaf_v, leaf_t, tree_v, tree_t], axis=0))
    leaf_full = gathered[:rows]
    leaf_tri = gathered[rows:rows + width]
    tree_full = gathered[rows + width:rows + 2 * width]
    tree_tri = gathered[rows + 2 * width:]

    leaf_vectors = unit_lower(leaf_full)
    leaf_factor = jnp.triu(leaf_tri)
    leaf_w = product_left_t(leaf_factor, product_left_t(leaf_vectors, slab))
    leafed = slab - product(leaf_vectors, leaf_w)
    current = leafed[:width]

    tree_vectors = jnp.triu(tree_full)
    tree_factor = jnp.triu(tree_tri)
    tree_joint = product(tree_vectors, tree_factor)
    own3 = jnp.stack([tree_vectors, tree_factor, tree_joint])

    core = position % 2
    base = position - core
    cols = slab.shape[1]
    half = cols // 2
    swap = [(p, p ^ 1) for p in range(n_row)]
    mate3 = lax.ppermute(own3, "row", swap)
    odd3 = jnp.where(core == 1, own3, mate3)
    even3 = jnp.where(core == 0, own3, mate3)

    partner_factors = []
    for level in range(1, levels):
        step = 1 << level
        pairs = []
        for i in range(0, n_row, 2 * step):
            pairs += [(i + step, i), (i + step + 1, i + 1)]
        partner_factors.append(lax.ppermute(even3[1:], "row", pairs))

    is_lower = core == 0
    received = lax.ppermute(current, "row", swap)
    own_h = lax.dynamic_slice(current, (0, core * half), (width, half))
    early = product_left_t(jnp.where(is_lower, odd3[1], odd3[2]), own_h)
    early, received = lax.optimization_barrier((early, received))
    recv_h = lax.dynamic_slice(received, (0, core * half), (width, half))
    update = early + product_left_t(jnp.where(is_lower, odd3[2], odd3[1]), recv_h)
    upper_h = jnp.where(is_lower, recv_h, own_h)
    level0_out = upper_h - product(odd3[0], update)
    chain = jnp.where(is_lower, own_h, recv_h) - update

    zeros = jnp.zeros_like(tree_factor)
    result = chain
    for level in range(1, levels):
        if level == 1:
            chain, partner_factors = lax.optimization_barrier((chain, partner_factors))
        step = 1 << level
        phase = base % (2 * step)
        is_lower = phase == 0
        is_upper = phase == step
        their = partner_factors[level - 1]
        first = jnp.where(is_lower, their[0], jnp.where(is_upper, even3[2], zeros))
        second = jnp.where(is_lower, their[1], jnp.where(is_upper, even3[1], zeros))
        pairs = []
        for i in range(0, n_row, 2 * step):
            for c in range(2):
                pairs += [(i + c, i + step + c), (i + step + c, i + c)]
        received = lax.ppermute(chain, "row", pairs)
        early = product_left_t(first, chain)
        early, received = lax.optimization_barrier((early, received))
        update = early + product_left_t(second, received)
        result = jnp.where(is_upper, chain - product(even3[0], update), result)
        chain = jnp.where(is_lower, chain - update, chain)
    base_out = jnp.where(base == 0, chain, result)

    keep = jnp.where(core == 0, base_out, level0_out)
    give = jnp.where(core == 0, level0_out, base_out)
    got = lax.ppermute(give, "row", swap)
    top = jnp.concatenate([jnp.where(core == 0, keep, got), jnp.where(core == 0, got, keep)], axis=1)
    return lax.dynamic_update_slice(leafed, top, (0, 0))


def solution(mesh):
    in_specs = (P("row", "col"), P("row", "col"), P("row", "col"), P("row", "col"), P("row", "col"))
    out_specs = P("row", "col")
    return jax.shard_map(
        on_device, mesh=mesh, in_specs=in_specs, out_specs=out_specs, check_vma=False
    )
```

```python
import jax
import jax.numpy as jnp
from jax import lax
from jax.sharding import PartitionSpec as P


def product(left, right):
    return jnp.dot(left, right, precision=lax.Precision.HIGHEST, preferred_element_type=jnp.float32)


def product_left_t(left, right):
    return lax.dot_general(
        left,
        right,
        (((0,), (0,)), ((), ())),
        precision=lax.Precision.HIGHEST,
        preferred_element_type=jnp.float32,
    )


def unit_lower(raw):
    row_ids = lax.broadcasted_iota(jnp.int32, raw.shape, 0)
    col_ids = lax.broadcasted_iota(jnp.int32, raw.shape, 1)
    diagonal = jnp.where(row_ids == col_ids, 1.0, 0.0).astype(raw.dtype)
    return jnp.where(row_ids > col_ids, raw, 0.0) + diagonal


def col_gather(part):
    n_col = lax.axis_size("col")
    me = lax.axis_index("col")
    by_shift = [part]
    for shift in range(1, n_col):
        perm = [(i, (i + shift) % n_col) for i in range(n_col)]
        by_shift.append(lax.ppermute(part, "col", perm))
    stacked = jnp.stack(by_shift)
    blocks = [stacked[(me - b) % n_col] for b in range(n_col)]
    return jnp.concatenate(blocks, axis=1)


def on_device(slab, leaf_v, leaf_t, tree_v, tree_t):
    n_row = lax.axis_size("row")
    levels = n_row.bit_length() - 1
    position = lax.axis_index("row")
    rows = leaf_v.shape[0]
    width = leaf_t.shape[0]

    gathered = col_gather(jnp.concatenate([leaf_v, leaf_t, tree_v, tree_t], axis=0))
    leaf_full = gathered[:rows]
    leaf_tri = gathered[rows:rows + width]
    tree_full = gathered[rows + width:rows + 2 * width]
    tree_tri = gathered[rows + 2 * width:]

    leaf_vectors = unit_lower(leaf_full)
    leaf_factor = jnp.triu(leaf_tri)
    leaf_w = product_left_t(leaf_factor, product_left_t(leaf_vectors, slab))
    leafed = slab - product(leaf_vectors, leaf_w)
    current = leafed[:width]

    tree_vectors = jnp.triu(tree_full)
    tree_factor = jnp.triu(tree_tri)
    tree_joint = product(tree_vectors, tree_factor)
    own3 = jnp.stack([tree_vectors, tree_factor, tree_joint])

    core = position % 2
    base = position - core
    cols = slab.shape[1]
    half = cols // 2
    swap = [(p, p ^ 1) for p in range(n_row)]
    mate3 = lax.ppermute(own3, "row", swap)
    odd3 = jnp.where(core == 1, own3, mate3)
    even3 = jnp.where(core == 0, own3, mate3)

    row_ids = lax.broadcasted_iota(jnp.int32, tree_factor.shape, 0)
    col_ids = lax.broadcasted_iota(jnp.int32, tree_factor.shape, 1)
    even_s, even_m = even3[1], even3[2]
    packed = jnp.where(row_ids <= col_ids, even_s, even_m.T)
    diag_m = jnp.sum(jnp.where(row_ids == col_ids, even_m, 0.0), axis=0, keepdims=True)
    packed = jnp.concatenate([packed, jnp.broadcast_to(diag_m, (8, width))], axis=0)
    partner_factors = []
    for level in range(1, levels):
        step = 1 << level
        pairs = []
        for i in range(0, n_row, 2 * step):
            pairs += [(i + step, i), (i + step + 1, i + 1)]
        partner_factors.append(lax.ppermute(packed, "row", pairs))

    def unpack(got):
        square = got[:width]
        their_s = jnp.where(row_ids <= col_ids, square, 0.0)
        their_m = jnp.where(row_ids < col_ids, square.T, jnp.where(row_ids == col_ids, got[width:width + 1], 0.0))
        return their_s, their_m

    is_lower = core == 0
    received = lax.ppermute(current, "row", swap)
    own_h = lax.dynamic_slice(current, (0, core * half), (width, half))
    early = product_left_t(jnp.where(is_lower, odd3[1], odd3[2]), own_h)
    early, received = lax.optimization_barrier((early, received))
    recv_h = lax.dynamic_slice(received, (0, core * half), (width, half))
    update = early + product_left_t(jnp.where(is_lower, odd3[2], odd3[1]), recv_h)
    upper_h = jnp.where(is_lower, recv_h, own_h)
    level0_out = upper_h - product(odd3[0], update)
    chain = jnp.where(is_lower, own_h, recv_h) - update

    zeros = jnp.zeros_like(tree_factor)
    result = chain
    for level in range(1, levels):
        if level == 1:
            chain, partner_factors[0] = lax.optimization_barrier((chain, partner_factors[0]))
        if level == 2:
            chain, rest = lax.optimization_barrier((chain, partner_factors[1:]))
            partner_factors[1:] = rest
        step = 1 << level
        phase = base % (2 * step)
        is_lower = phase == 0
        is_upper = phase == step
        their = unpack(partner_factors[level - 1])
        first = jnp.where(is_lower, their[0], jnp.where(is_upper, even3[2], zeros))
        second = jnp.where(is_lower, their[1], jnp.where(is_upper, even3[1], zeros))
        pairs = []
        for i in range(0, n_row, 2 * step):
            for c in range(2):
                pairs += [(i + c, i + step + c), (i + step + c, i + c)]
        received = lax.ppermute(chain, "row", pairs)
        early = product_left_t(first, chain)
        early, received = lax.optimization_barrier((early, received))
        update = early + product_left_t(second, received)
        result = jnp.where(is_upper, chain - product(even3[0], update), result)
        chain = jnp.where(is_lower, chain - update, chain)
    base_out = jnp.where(base == 0, chain, result)

    keep = jnp.where(core == 0, base_out, level0_out)
    give = jnp.where(core == 0, level0_out, base_out)
    got = lax.ppermute(give, "row", swap)
    top = jnp.concatenate([jnp.where(core == 0, keep, got), jnp.where(core == 0, got, keep)], axis=1)
    return jnp.concatenate([top, leafed[width:]], axis=0)


def solution(mesh):
    in_specs = (P("row", "col"), P("row", "col"), P("row", "col"), P("row", "col"), P("row", "col"))
    out_specs = P("row", "col")
    return jax.shard_map(
        on_device, mesh=mesh, in_specs=in_specs, out_specs=out_specs, check_vma=False
    )
```

```python
import jax
import jax.numpy as jnp
from jax import lax
from jax.sharding import PartitionSpec as P


def product(left, right):
    return jnp.dot(left, right, precision=lax.Precision.HIGHEST, preferred_element_type=jnp.float32)


def product_left_t(left, right):
    return lax.dot_general(
        left,
        right,
        (((0,), (0,)), ((), ())),
        precision=lax.Precision.HIGHEST,
        preferred_element_type=jnp.float32,
    )


def unit_lower(raw):
    row_ids = lax.broadcasted_iota(jnp.int32, raw.shape, 0)
    col_ids = lax.broadcasted_iota(jnp.int32, raw.shape, 1)
    diagonal = jnp.where(row_ids == col_ids, 1.0, 0.0).astype(raw.dtype)
    return jnp.where(row_ids > col_ids, raw, 0.0) + diagonal


def col_gather(part):
    n_col = lax.axis_size("col")
    me = lax.axis_index("col")
    by_shift = [part]
    for shift in range(1, n_col):
        perm = [(i, (i + shift) % n_col) for i in range(n_col)]
        by_shift.append(lax.ppermute(part, "col", perm))
    stacked = jnp.stack(by_shift)
    blocks = [stacked[(me - b) % n_col] for b in range(n_col)]
    return jnp.concatenate(blocks, axis=1)


def on_device(slab, leaf_v, leaf_t, tree_v, tree_t):
    n_row = lax.axis_size("row")
    levels = n_row.bit_length() - 1
    position = lax.axis_index("row")
    rows = leaf_v.shape[0]
    width = leaf_t.shape[0]

    tree_gathered = col_gather(jnp.concatenate([tree_v, tree_t], axis=0))
    tree_gathered, leaf_v, leaf_t = lax.optimization_barrier((tree_gathered, leaf_v, leaf_t))
    leaf_gathered = col_gather(jnp.concatenate([leaf_v, leaf_t], axis=0))
    leaf_full = leaf_gathered[:rows]
    leaf_tri = leaf_gathered[rows:]
    tree_full = tree_gathered[:width]
    tree_tri = tree_gathered[width:]

    tree_vectors = jnp.triu(tree_full)
    tree_factor = jnp.triu(tree_tri)
    tree_joint = product(tree_vectors, tree_factor)
    own3 = jnp.stack([tree_vectors, tree_factor, tree_joint])

    core = position % 2
    base = position - core
    cols = slab.shape[1]
    half = cols // 2
    swap = [(p, p ^ 1) for p in range(n_row)]
    mate3 = lax.ppermute(own3, "row", swap)
    odd3 = jnp.where(core == 1, own3, mate3)
    even3 = jnp.where(core == 0, own3, mate3)

    row_ids = lax.broadcasted_iota(jnp.int32, tree_factor.shape, 0)
    col_ids = lax.broadcasted_iota(jnp.int32, tree_factor.shape, 1)
    even_s, even_m = even3[1], even3[2]
    packed = jnp.where(row_ids <= col_ids, even_s, even_m.T)
    diag_m = jnp.sum(jnp.where(row_ids == col_ids, even_m, 0.0), axis=0, keepdims=True)
    packed = jnp.concatenate([packed, jnp.broadcast_to(diag_m, (8, width))], axis=0)
    partner_factors = []
    for level in range(1, levels):
        step = 1 << level
        pairs = []
        for i in range(0, n_row, 2 * step):
            pairs += [(i + step, i), (i + step + 1, i + 1)]
        partner_factors.append(lax.ppermute(packed, "row", pairs))

    def unpack(got):
        square = got[:width]
        their_s = jnp.where(row_ids <= col_ids, square, 0.0)
        their_m = jnp.where(row_ids < col_ids, square.T, jnp.where(row_ids == col_ids, got[width:width + 1], 0.0))
        return their_s, their_m

    leaf_full, leaf_tri, partner_factors[0] = lax.optimization_barrier((leaf_full, leaf_tri, partner_factors[0]))
    leaf_vectors = unit_lower(leaf_full)
    leaf_factor = jnp.triu(leaf_tri)
    leaf_w = product_left_t(leaf_factor, product_left_t(leaf_vectors, slab))
    leafed = slab - product(leaf_vectors, leaf_w)
    current = leafed[:width]

    is_lower = core == 0
    received = lax.ppermute(current, "row", swap)
    own_h = lax.dynamic_slice(current, (0, core * half), (width, half))
    early = product_left_t(jnp.where(is_lower, odd3[1], odd3[2]), own_h)
    early, received = lax.optimization_barrier((early, received))
    recv_h = lax.dynamic_slice(received, (0, core * half), (width, half))
    update = early + product_left_t(jnp.where(is_lower, odd3[2], odd3[1]), recv_h)
    upper_h = jnp.where(is_lower, recv_h, own_h)
    level0_out = upper_h - product(odd3[0], update)
    chain = jnp.where(is_lower, own_h, recv_h) - update

    zeros = jnp.zeros_like(tree_factor)
    result = chain
    for level in range(1, levels):
        if level == 2:
            chain, rest = lax.optimization_barrier((chain, partner_factors[1:]))
            partner_factors[1:] = rest
        step = 1 << level
        phase = base % (2 * step)
        is_lower = phase == 0
        is_upper = phase == step
        their = unpack(partner_factors[level - 1])
        first = jnp.where(is_lower, their[0], jnp.where(is_upper, even3[2], zeros))
        second = jnp.where(is_lower, their[1], jnp.where(is_upper, even3[1], zeros))
        pairs = []
        for i in range(0, n_row, 2 * step):
            for c in range(2):
                pairs += [(i + c, i + step + c), (i + step + c, i + c)]
        received = lax.ppermute(chain, "row", pairs)
        early = product_left_t(first, chain)
        early, received = lax.optimization_barrier((early, received))
        update = early + product_left_t(second, received)
        result = jnp.where(is_upper, chain - product(even3[0], update), result)
        chain = jnp.where(is_lower, chain - update, chain)
    base_out = jnp.where(base == 0, chain, result)

    keep = jnp.where(core == 0, base_out, level0_out)
    give = jnp.where(core == 0, level0_out, base_out)
    got = lax.ppermute(give, "row", swap)
    top = jnp.concatenate([jnp.where(core == 0, keep, got), jnp.where(core == 0, got, keep)], axis=1)
    return jnp.concatenate([top, leafed[width:]], axis=0)


def solution(mesh):
    in_specs = (P("row", "col"), P("row", "col"), P("row", "col"), P("row", "col"), P("row", "col"))
    out_specs = P("row", "col")
    return jax.shard_map(
        on_device, mesh=mesh, in_specs=in_specs, out_specs=out_specs, check_vma=False
    )
```

```python
import jax
import jax.numpy as jnp
from jax import lax
from jax.sharding import PartitionSpec as P


def product(left, right):
    return jnp.dot(left, right, precision=lax.Precision.HIGHEST, preferred_element_type=jnp.float32)


def product_left_t(left, right):
    return lax.dot_general(
        left,
        right,
        (((0,), (0,)), ((), ())),
        precision=lax.Precision.HIGHEST,
        preferred_element_type=jnp.float32,
    )


def unit_lower(raw):
    row_ids = lax.broadcasted_iota(jnp.int32, raw.shape, 0)
    col_ids = lax.broadcasted_iota(jnp.int32, raw.shape, 1)
    diagonal = jnp.where(row_ids == col_ids, 1.0, 0.0).astype(raw.dtype)
    return jnp.where(row_ids > col_ids, raw, 0.0) + diagonal


def col_gather(part):
    n_col = lax.axis_size("col")
    me = lax.axis_index("col")
    by_shift = [part]
    for shift in range(1, n_col):
        perm = [(i, (i + shift) % n_col) for i in range(n_col)]
        by_shift.append(lax.ppermute(part, "col", perm))
    stacked = jnp.stack(by_shift)
    blocks = [stacked[(me - b) % n_col] for b in range(n_col)]
    return jnp.concatenate(blocks, axis=1)


def on_device(slab, leaf_v, leaf_t, tree_v, tree_t):
    n_row = lax.axis_size("row")
    levels = n_row.bit_length() - 1
    position = lax.axis_index("row")
    rows = leaf_v.shape[0]
    width = leaf_t.shape[0]

    gathered = col_gather(jnp.concatenate([leaf_v, leaf_t, tree_v, tree_t], axis=0))
    leaf_full = gathered[:rows]
    leaf_tri = gathered[rows:rows + width]
    tree_full = gathered[rows + width:rows + 2 * width]
    tree_tri = gathered[rows + 2 * width:]

    leaf_vectors = unit_lower(leaf_full)
    leaf_factor = jnp.triu(leaf_tri)
    leaf_w = product_left_t(leaf_factor, product_left_t(leaf_vectors, slab))
    leafed = slab - product(leaf_vectors, leaf_w)
    current = leafed[:width]

    tree_vectors = jnp.triu(tree_full)
    tree_factor = jnp.triu(tree_tri)
    tree_joint = product(tree_vectors, tree_factor)
    own3 = jnp.stack([tree_vectors, tree_factor, tree_joint])

    core = position % 2
    base = position - core
    cols = slab.shape[1]
    half = cols // 2
    swap = [(p, p ^ 1) for p in range(n_row)]
    mate3 = lax.ppermute(own3, "row", swap)
    odd3 = jnp.where(core == 1, own3, mate3)
    even3 = jnp.where(core == 0, own3, mate3)

    hw = width // 2
    sub_r = lax.broadcasted_iota(jnp.int32, (hw, hw), 0)
    sub_c = lax.broadcasted_iota(jnp.int32, (hw, hw), 1)
    even_s = even3[1]
    corner = even_s[hw:, hw:]
    folded = jnp.where(sub_r <= sub_c, even_s[:hw, :hw], corner.T)
    corner_diag = jnp.sum(jnp.where(sub_r == sub_c, corner, 0.0), axis=0, keepdims=True)
    packed = jnp.concatenate(
        [
            jnp.concatenate([folded, even_s[:hw, hw:]], axis=1),
            jnp.broadcast_to(jnp.concatenate([corner_diag, jnp.zeros_like(corner_diag)], axis=1), (8, width)),
        ],
        axis=0,
    )
    partner_factors = []
    for level in range(1, levels):
        step = 1 << level
        pairs = []
        for i in range(0, n_row, 2 * step):
            pairs += [(i + step, i), (i + step + 1, i + 1)]
        partner_factors.append(lax.ppermute(packed, "row", pairs))

    def unpack(got):
        square = got[:hw, :hw]
        top_left = jnp.where(sub_r <= sub_c, square, 0.0)
        bottom_right = jnp.where(sub_r < sub_c, square.T, jnp.where(sub_r == sub_c, got[hw:hw + 1, :hw], 0.0))
        top = jnp.concatenate([top_left, got[:hw, hw:]], axis=1)
        bottom = jnp.concatenate([jnp.zeros_like(bottom_right), bottom_right], axis=1)
        return jnp.concatenate([top, bottom], axis=0)

    is_lower = core == 0
    received = lax.ppermute(current, "row", swap)
    own_h = lax.dynamic_slice(current, (0, core * half), (width, half))
    early = product_left_t(jnp.where(is_lower, odd3[1], odd3[2]), own_h)
    early, received = lax.optimization_barrier((early, received))
    recv_h = lax.dynamic_slice(received, (0, core * half), (width, half))
    update = early + product_left_t(jnp.where(is_lower, odd3[2], odd3[1]), recv_h)
    upper_h = jnp.where(is_lower, recv_h, own_h)
    level0_out = upper_h - product(odd3[0], update)
    chain = jnp.where(is_lower, own_h, recv_h) - update

    zeros = jnp.zeros_like(tree_factor)
    result = chain
    for level in range(1, levels):
        if level == 1:
            chain, partner_factors[0] = lax.optimization_barrier((chain, partner_factors[0]))
        if level == 2:
            chain, rest = lax.optimization_barrier((chain, partner_factors[1:]))
            partner_factors[1:] = rest
        step = 1 << level
        phase = base % (2 * step)
        is_lower = phase == 0
        is_upper = phase == step
        their_s = unpack(partner_factors[level - 1])
        first = jnp.where(is_lower, their_s, jnp.where(is_upper, even3[2], zeros))
        pairs = []
        for i in range(0, n_row, 2 * step):
            for c in range(2):
                pairs += [(i + c, i + step + c), (i + step + c, i + c)]
        early = product_left_t(first, chain)
        received = lax.ppermute(jnp.where(is_upper, early, chain), "row", pairs)
        update = product_left_t(even3[1], received) + early
        result = jnp.where(is_upper, chain - product(even3[0], update), result)
        chain = jnp.where(is_lower, chain - early - received, chain)
    base_out = jnp.where(base == 0, chain, result)

    keep = jnp.where(core == 0, base_out, level0_out)
    give = jnp.where(core == 0, level0_out, base_out)
    got = lax.ppermute(give, "row", swap)
    top = jnp.concatenate([jnp.where(core == 0, keep, got), jnp.where(core == 0, got, keep)], axis=1)
    return jnp.concatenate([top, leafed[width:]], axis=0)


def solution(mesh):
    in_specs = (P("row", "col"), P("row", "col"), P("row", "col"), P("row", "col"), P("row", "col"))
    out_specs = P("row", "col")
    return jax.shard_map(
        on_device, mesh=mesh, in_specs=in_specs, out_specs=out_specs, check_vma=False
    )
```

```python
import jax
import jax.numpy as jnp
from jax import lax
from jax.sharding import PartitionSpec as P


def product(left, right):
    return jnp.dot(left, right, precision=lax.Precision.HIGH, preferred_element_type=jnp.float32)


def product_left_t(left, right):
    return lax.dot_general(
        left,
        right,
        (((0,), (0,)), ((), ())),
        precision=lax.Precision.HIGH,
        preferred_element_type=jnp.float32,
    )


def unit_lower(raw):
    row_ids = lax.broadcasted_iota(jnp.int32, raw.shape, 0)
    col_ids = lax.broadcasted_iota(jnp.int32, raw.shape, 1)
    diagonal = jnp.where(row_ids == col_ids, 1.0, 0.0).astype(raw.dtype)
    return jnp.where(row_ids > col_ids, raw, 0.0) + diagonal


def col_gather(part):
    n_col = lax.axis_size("col")
    me = lax.axis_index("col")
    by_shift = [part]
    for shift in range(1, n_col):
        perm = [(i, (i + shift) % n_col) for i in range(n_col)]
        by_shift.append(lax.ppermute(part, "col", perm))
    stacked = jnp.stack(by_shift)
    blocks = [stacked[(me - b) % n_col] for b in range(n_col)]
    return jnp.concatenate(blocks, axis=1)


def on_device(slab, leaf_v, leaf_t, tree_v, tree_t):
    n_row = lax.axis_size("row")
    levels = n_row.bit_length() - 1
    position = lax.axis_index("row")
    rows = leaf_v.shape[0]
    width = leaf_t.shape[0]

    gathered = col_gather(jnp.concatenate([leaf_v, leaf_t, tree_v, tree_t], axis=0))
    leaf_full = gathered[:rows]
    leaf_tri = gathered[rows:rows + width]
    tree_full = gathered[rows + width:rows + 2 * width]
    tree_tri = gathered[rows + 2 * width:]

    leaf_vectors = unit_lower(leaf_full)
    leaf_factor = jnp.triu(leaf_tri)
    leaf_w = product_left_t(leaf_factor, product_left_t(leaf_vectors, slab))
    leafed = slab - product(leaf_vectors, leaf_w)
    current = leafed[:width]

    tree_vectors = jnp.triu(tree_full)
    tree_factor = jnp.triu(tree_tri)
    tree_joint = product(tree_vectors, tree_factor)
    own3 = jnp.stack([tree_vectors, tree_factor, tree_joint])

    core = position % 2
    base = position - core
    cols = slab.shape[1]
    half = cols // 2
    swap = [(p, p ^ 1) for p in range(n_row)]
    mate3 = lax.ppermute(own3, "row", swap)
    odd3 = jnp.where(core == 1, own3, mate3)
    even3 = jnp.where(core == 0, own3, mate3)

    hw = width // 2
    sub_r = lax.broadcasted_iota(jnp.int32, (hw, hw), 0)
    sub_c = lax.broadcasted_iota(jnp.int32, (hw, hw), 1)
    even_s = even3[1]
    corner = even_s[hw:, hw:]
    folded = jnp.where(sub_r <= sub_c, even_s[:hw, :hw], corner.T)
    corner_diag = jnp.sum(jnp.where(sub_r == sub_c, corner, 0.0), axis=0, keepdims=True)
    packed = jnp.concatenate(
        [
            jnp.concatenate([folded, even_s[:hw, hw:]], axis=1),
            jnp.broadcast_to(jnp.concatenate([corner_diag, jnp.zeros_like(corner_diag)], axis=1), (8, width)),
        ],
        axis=0,
    )
    partner_factors = []
    for level in range(1, levels):
        step = 1 << level
        pairs = []
        for i in range(0, n_row, 2 * step):
            pairs += [(i + step, i), (i + step + 1, i + 1)]
        partner_factors.append(lax.ppermute(packed, "row", pairs))

    def unpack(got):
        square = got[:hw, :hw]
        top_left = jnp.where(sub_r <= sub_c, square, 0.0)
        bottom_right = jnp.where(sub_r < sub_c, square.T, jnp.where(sub_r == sub_c, got[hw:hw + 1, :hw], 0.0))
        top = jnp.concatenate([top_left, got[:hw, hw:]], axis=1)
        bottom = jnp.concatenate([jnp.zeros_like(bottom_right), bottom_right], axis=1)
        return jnp.concatenate([top, bottom], axis=0)

    is_lower = core == 0
    received = lax.ppermute(current, "row", swap)
    own_h = lax.dynamic_slice(current, (0, core * half), (width, half))
    early = product_left_t(jnp.where(is_lower, odd3[1], odd3[2]), own_h)
    early, received = lax.optimization_barrier((early, received))
    recv_h = lax.dynamic_slice(received, (0, core * half), (width, half))
    update = early + product_left_t(jnp.where(is_lower, odd3[2], odd3[1]), recv_h)
    upper_h = jnp.where(is_lower, recv_h, own_h)
    level0_out = upper_h - product(odd3[0], update)
    chain = jnp.where(is_lower, own_h, recv_h) - update

    zeros = jnp.zeros_like(tree_factor)
    result = chain
    for level in range(1, levels):
        if level == 1:
            chain, partner_factors[0] = lax.optimization_barrier((chain, partner_factors[0]))
        if level == 2:
            chain, rest = lax.optimization_barrier((chain, partner_factors[1:]))
            partner_factors[1:] = rest
        step = 1 << level
        phase = base % (2 * step)
        is_lower = phase == 0
        is_upper = phase == step
        their_s = unpack(partner_factors[level - 1])
        first = jnp.where(is_lower, their_s, jnp.where(is_upper, even3[2], zeros))
        pairs = []
        for i in range(0, n_row, 2 * step):
            for c in range(2):
                pairs += [(i + c, i + step + c), (i + step + c, i + c)]
        early = product_left_t(first, chain)
        received = lax.ppermute(jnp.where(is_upper, early, chain), "row", pairs)
        update = product_left_t(even3[1], received) + early
        result = jnp.where(is_upper, chain - product(even3[0], update), result)
        chain = jnp.where(is_lower, chain - early - received, chain)
    base_out = jnp.where(base == 0, chain, result)

    keep = jnp.where(core == 0, base_out, level0_out)
    give = jnp.where(core == 0, level0_out, base_out)
    got = lax.ppermute(give, "row", swap)
    top = jnp.concatenate([jnp.where(core == 0, keep, got), jnp.where(core == 0, got, keep)], axis=1)
    return jnp.concatenate([top, leafed[width:]], axis=0)


def solution(mesh):
    in_specs = (P("row", "col"), P("row", "col"), P("row", "col"), P("row", "col"), P("row", "col"))
    out_specs = P("row", "col")
    return jax.shard_map(
        on_device, mesh=mesh, in_specs=in_specs, out_specs=out_specs, check_vma=False
    )
```

```python
import jax
import jax.numpy as jnp
from jax import lax
from jax.sharding import PartitionSpec as P


def product(left, right):
    return jnp.dot(left, right, precision=lax.Precision.HIGH, preferred_element_type=jnp.float32)


def product_left_t(left, right):
    return lax.dot_general(
        left,
        right,
        (((0,), (0,)), ((), ())),
        precision=lax.Precision.HIGH,
        preferred_element_type=jnp.float32,
    )


def unit_lower(raw):
    row_ids = lax.broadcasted_iota(jnp.int32, raw.shape, 0)
    col_ids = lax.broadcasted_iota(jnp.int32, raw.shape, 1)
    diagonal = jnp.where(row_ids == col_ids, 1.0, 0.0).astype(raw.dtype)
    return jnp.where(row_ids > col_ids, raw, 0.0) + diagonal


def col_gather(part):
    n_col = lax.axis_size("col")
    me = lax.axis_index("col")
    by_shift = [part]
    for shift in range(1, n_col):
        perm = [(i, (i + shift) % n_col) for i in range(n_col)]
        by_shift.append(lax.ppermute(part, "col", perm))
    stacked = jnp.stack(by_shift)
    blocks = [stacked[(me - b) % n_col] for b in range(n_col)]
    return jnp.concatenate(blocks, axis=1)


def on_device(slab, leaf_v, leaf_t, tree_v, tree_t):
    n_row = lax.axis_size("row")
    levels = n_row.bit_length() - 1
    position = lax.axis_index("row")
    rows = leaf_v.shape[0]
    width = leaf_t.shape[0]

    gathered = col_gather(jnp.concatenate([leaf_v, leaf_t, tree_v, tree_t], axis=0))
    leaf_full = gathered[:rows]
    leaf_tri = gathered[rows:rows + width]
    tree_full = gathered[rows + width:rows + 2 * width]
    tree_tri = gathered[rows + 2 * width:]

    leaf_vectors = unit_lower(leaf_full)
    leaf_factor = jnp.triu(leaf_tri)
    leaf_w = product_left_t(leaf_factor, product_left_t(leaf_vectors, slab))
    leafed = slab - product(leaf_vectors, leaf_w)
    current = leafed[:width]

    tree_vectors = jnp.triu(tree_full)
    tree_factor = jnp.triu(tree_tri)
    tree_joint = product(tree_vectors, tree_factor)
    own3 = jnp.stack([tree_vectors, tree_factor, tree_joint])

    core = position % 2
    base = position - core
    cols = slab.shape[1]
    half = cols // 2
    swap = [(p, p ^ 1) for p in range(n_row)]
    mate3 = lax.ppermute(own3, "row", swap)
    odd3 = jnp.where(core == 1, own3, mate3)
    even3 = jnp.where(core == 0, own3, mate3)

    hw = width // 2
    sub_r = lax.broadcasted_iota(jnp.int32, (hw, hw), 0)
    sub_c = lax.broadcasted_iota(jnp.int32, (hw, hw), 1)
    even_s = even3[1]
    corner = even_s[hw:, hw:]
    folded = jnp.where(sub_r <= sub_c, even_s[:hw, :hw], corner.T)
    corner_diag = jnp.sum(jnp.where(sub_r == sub_c, corner, 0.0), axis=0, keepdims=True)
    packed = jnp.concatenate(
        [
            jnp.concatenate([folded, even_s[:hw, hw:]], axis=1),
            jnp.broadcast_to(jnp.concatenate([corner_diag, jnp.zeros_like(corner_diag)], axis=1), (8, width)),
        ],
        axis=0,
    )
    partner_factors = []
    for level in range(1, levels):
        step = 1 << level
        pairs = []
        for i in range(0, n_row, 2 * step):
            pairs += [(i + step, i), (i + step + 1, i + 1)]
        partner_factors.append(lax.ppermute(packed, "row", pairs))

    def unpack(got):
        square = got[:hw, :hw]
        top_left = jnp.where(sub_r <= sub_c, square, 0.0)
        bottom_right = jnp.where(sub_r < sub_c, square.T, jnp.where(sub_r == sub_c, got[hw:hw + 1, :hw], 0.0))
        top = jnp.concatenate([top_left, got[:hw, hw:]], axis=1)
        bottom = jnp.concatenate([jnp.zeros_like(bottom_right), bottom_right], axis=1)
        return jnp.concatenate([top, bottom], axis=0)

    is_lower = core == 0
    received = lax.ppermute(current, "row", swap)
    own_h = lax.dynamic_slice(current, (0, core * half), (width, half))
    early = product_left_t(jnp.where(is_lower, odd3[1], odd3[2]), own_h)
    early, received, partner_factors[0] = lax.optimization_barrier((early, received, partner_factors[0]))
    recv_h = lax.dynamic_slice(received, (0, core * half), (width, half))
    update = early + product_left_t(jnp.where(is_lower, odd3[2], odd3[1]), recv_h)
    upper_h = jnp.where(is_lower, recv_h, own_h)
    level0_out = upper_h - product(odd3[0], update)
    chain = jnp.where(is_lower, own_h, recv_h) - update

    zeros = jnp.zeros_like(tree_factor)
    result = chain
    for level in range(1, levels):
        step = 1 << level
        phase = base % (2 * step)
        is_lower = phase == 0
        is_upper = phase == step
        pairs = []
        for i in range(0, n_row, 2 * step):
            for c in range(2):
                pairs += [(i + c, i + step + c), (i + step + c, i + c)]
        q = product_left_t(jnp.where(is_upper, even3[2], zeros), chain)
        received = lax.ppermute(jnp.where(is_upper, q, chain), "row", pairs)
        if level == 1:
            received, rest = lax.optimization_barrier((received, partner_factors[1:]))
            partner_factors[1:] = rest
        their_s = unpack(partner_factors[level - 1])
        own_part = product_left_t(jnp.where(is_lower, their_s, zeros), chain)
        update = product_left_t(even3[1], received) + q
        result = jnp.where(is_upper, chain - product(even3[0], update), result)
        chain = jnp.where(is_lower, chain - own_part - received, chain)
    base_out = jnp.where(base == 0, chain, result)

    keep = jnp.where(core == 0, base_out, level0_out)
    give = jnp.where(core == 0, level0_out, base_out)
    got = lax.ppermute(give, "row", swap)
    top = jnp.concatenate([jnp.where(core == 0, keep, got), jnp.where(core == 0, got, keep)], axis=1)
    return jnp.concatenate([top, leafed[width:]], axis=0)


def solution(mesh):
    in_specs = (P("row", "col"), P("row", "col"), P("row", "col"), P("row", "col"), P("row", "col"))
    out_specs = P("row", "col")
    return jax.shard_map(
        on_device, mesh=mesh, in_specs=in_specs, out_specs=out_specs, check_vma=False
    )
```

```python
import jax
import jax.numpy as jnp
from jax import lax
from jax.sharding import PartitionSpec as P


def product(left, right):
    return jnp.dot(left, right, precision=lax.Precision.HIGH, preferred_element_type=jnp.float32)


def product_left_t(left, right):
    return lax.dot_general(
        left,
        right,
        (((0,), (0,)), ((), ())),
        precision=lax.Precision.HIGH,
        preferred_element_type=jnp.float32,
    )


def unit_lower(raw):
    row_ids = lax.broadcasted_iota(jnp.int32, raw.shape, 0)
    col_ids = lax.broadcasted_iota(jnp.int32, raw.shape, 1)
    diagonal = jnp.where(row_ids == col_ids, 1.0, 0.0).astype(raw.dtype)
    return jnp.where(row_ids > col_ids, raw, 0.0) + diagonal


def col_gather(part):
    n_col = lax.axis_size("col")
    me = lax.axis_index("col")
    by_shift = [part]
    for shift in range(1, n_col):
        perm = [(i, (i + shift) % n_col) for i in range(n_col)]
        by_shift.append(lax.ppermute(part, "col", perm))
    stacked = jnp.stack(by_shift)
    blocks = [stacked[(me - b) % n_col] for b in range(n_col)]
    return jnp.concatenate(blocks, axis=1)


def on_device(slab, leaf_v, leaf_t, tree_v, tree_t):
    n_row = lax.axis_size("row")
    levels = n_row.bit_length() - 1
    position = lax.axis_index("row")
    rows = leaf_v.shape[0]
    width = leaf_t.shape[0]

    gathered = col_gather(jnp.concatenate([leaf_v, leaf_t, tree_v, tree_t], axis=0))
    leaf_full = gathered[:rows]
    leaf_tri = gathered[rows:rows + width]
    tree_full = gathered[rows + width:rows + 2 * width]
    tree_tri = gathered[rows + 2 * width:]

    leaf_vectors = unit_lower(leaf_full)
    leaf_factor = jnp.triu(leaf_tri)
    leaf_w = product_left_t(leaf_factor, product_left_t(leaf_vectors, slab))
    leafed = slab - product(leaf_vectors, leaf_w)
    current = leafed[:width]

    tree_vectors = jnp.triu(tree_full)
    tree_factor = jnp.triu(tree_tri)
    tree_joint = product(tree_vectors, tree_factor)
    own3 = jnp.stack([tree_vectors, tree_factor, tree_joint])

    core = position % 2
    base = position - core
    cols = slab.shape[1]
    half = cols // 2
    swap = [(p, p ^ 1) for p in range(n_row)]
    mate3 = lax.ppermute(own3, "row", swap)
    odd3 = jnp.where(core == 1, own3, mate3)
    even3 = jnp.where(core == 0, own3, mate3)

    packed = even3[1]
    partner_factors = []
    for level in range(1, levels):
        step = 1 << level
        pairs = []
        for i in range(0, n_row, 2 * step):
            pairs += [(i + step, i), (i + step + 1, i + 1)]
        partner_factors.append(lax.ppermute(packed, "row", pairs))

    is_lower = core == 0
    received = lax.ppermute(current, "row", swap)
    own_h = lax.dynamic_slice(current, (0, core * half), (width, half))
    early = product_left_t(jnp.where(is_lower, odd3[1], odd3[2]), own_h)
    early, received, partner_factors[0] = lax.optimization_barrier((early, received, partner_factors[0]))
    recv_h = lax.dynamic_slice(received, (0, core * half), (width, half))
    update = early + product_left_t(jnp.where(is_lower, odd3[2], odd3[1]), recv_h)
    upper_h = jnp.where(is_lower, recv_h, own_h)
    level0_out = upper_h - product(odd3[0], update)
    chain = jnp.where(is_lower, own_h, recv_h) - update

    zeros = jnp.zeros_like(tree_factor)
    result = chain
    for level in range(1, levels):
        step = 1 << level
        phase = base % (2 * step)
        is_lower = phase == 0
        is_upper = phase == step
        pairs = []
        for i in range(0, n_row, 2 * step):
            for c in range(2):
                pairs += [(i + c, i + step + c), (i + step + c, i + c)]
        q = product_left_t(jnp.where(is_upper, even3[2], zeros), chain)
        received = lax.ppermute(jnp.where(is_upper, q, chain), "row", pairs)
        if level == 1:
            received, rest = lax.optimization_barrier((received, partner_factors[1:]))
            partner_factors[1:] = rest
        their_s = partner_factors[level - 1]
        own_part = product_left_t(jnp.where(is_lower, their_s, zeros), chain)
        update = product_left_t(even3[1], received) + q
        result = jnp.where(is_upper, chain - product(even3[0], update), result)
        chain = jnp.where(is_lower, chain - own_part - received, chain)
    base_out = jnp.where(base == 0, chain, result)

    keep = jnp.where(core == 0, base_out, level0_out)
    give = jnp.where(core == 0, level0_out, base_out)
    got = lax.ppermute(give, "row", swap)
    top = jnp.concatenate([jnp.where(core == 0, keep, got), jnp.where(core == 0, got, keep)], axis=1)
    return jnp.concatenate([top, leafed[width:]], axis=0)


def solution(mesh):
    in_specs = (P("row", "col"), P("row", "col"), P("row", "col"), P("row", "col"), P("row", "col"))
    out_specs = P("row", "col")
    return jax.shard_map(
        on_device, mesh=mesh, in_specs=in_specs, out_specs=out_specs, check_vma=False
    )
```

```python
import jax
import jax.numpy as jnp
from jax import lax
from jax.sharding import PartitionSpec as P


def product(left, right):
    return jnp.dot(left, right, precision=lax.Precision.HIGH, preferred_element_type=jnp.float32)


def product_left_t(left, right):
    return lax.dot_general(
        left,
        right,
        (((0,), (0,)), ((), ())),
        precision=lax.Precision.HIGH,
        preferred_element_type=jnp.float32,
    )


def unit_lower(raw):
    row_ids = lax.broadcasted_iota(jnp.int32, raw.shape, 0)
    col_ids = lax.broadcasted_iota(jnp.int32, raw.shape, 1)
    diagonal = jnp.where(row_ids == col_ids, 1.0, 0.0).astype(raw.dtype)
    return jnp.where(row_ids > col_ids, raw, 0.0) + diagonal


def col_gather(part):
    n_col = lax.axis_size("col")
    me = lax.axis_index("col")
    by_shift = [part]
    for shift in range(1, n_col):
        perm = [(i, (i + shift) % n_col) for i in range(n_col)]
        by_shift.append(lax.ppermute(part, "col", perm))
    stacked = jnp.stack(by_shift)
    blocks = [stacked[(me - b) % n_col] for b in range(n_col)]
    return jnp.concatenate(blocks, axis=1)


def on_device(slab, leaf_v, leaf_t, tree_v, tree_t):
    n_row = lax.axis_size("row")
    levels = n_row.bit_length() - 1
    position = lax.axis_index("row")
    rows = leaf_v.shape[0]
    width = leaf_t.shape[0]

    gathered = col_gather(jnp.concatenate([leaf_v, leaf_t, tree_v, tree_t], axis=0))
    leaf_full = gathered[:rows]
    leaf_tri = gathered[rows:rows + width]
    tree_full = gathered[rows + width:rows + 2 * width]
    tree_tri = gathered[rows + 2 * width:]

    leaf_vectors = unit_lower(leaf_full)
    leaf_factor = jnp.triu(leaf_tri)
    leaf_w = product_left_t(leaf_factor, product_left_t(leaf_vectors, slab))
    leafed = slab - product(leaf_vectors, leaf_w)
    current = leafed[:width]

    tree_vectors = jnp.triu(tree_full)
    tree_factor = jnp.triu(tree_tri)
    tree_joint = product(tree_vectors, tree_factor)
    own3 = jnp.stack([tree_vectors, tree_factor, tree_joint])

    core = position % 2
    base = position - core
    cols = slab.shape[1]
    half = cols // 2
    swap = [(p, p ^ 1) for p in range(n_row)]
    mate3 = lax.ppermute(own3, "row", swap)
    odd3 = jnp.where(core == 1, own3, mate3)
    even3 = jnp.where(core == 0, own3, mate3)

    packed = even3[1]
    partner_factors = []
    for level in range(1, levels):
        step = 1 << level
        pairs = []
        for i in range(0, n_row, 2 * step):
            pairs += [(i + step, i), (i + step + 1, i + 1)]
        if level == 2:
            partner_factors[0], packed = lax.optimization_barrier((partner_factors[0], packed))
        partner_factors.append(lax.ppermute(packed, "row", pairs))

    is_lower = core == 0
    received = lax.ppermute(current, "row", swap)
    own_h = lax.dynamic_slice(current, (0, core * half), (width, half))
    early = product_left_t(jnp.where(is_lower, odd3[1], odd3[2]), own_h)
    early, received, partner_factors[0] = lax.optimization_barrier((early, received, partner_factors[0]))
    recv_h = lax.dynamic_slice(received, (0, core * half), (width, half))
    update = early + product_left_t(jnp.where(is_lower, odd3[2], odd3[1]), recv_h)
    upper_h = jnp.where(is_lower, recv_h, own_h)
    level0_out = upper_h - product(odd3[0], update)
    chain = jnp.where(is_lower, own_h, recv_h) - update

    zeros = jnp.zeros_like(tree_factor)
    result = chain
    for level in range(1, levels):
        step = 1 << level
        phase = base % (2 * step)
        is_lower = phase == 0
        is_upper = phase == step
        pairs = []
        for i in range(0, n_row, 2 * step):
            for c in range(2):
                pairs += [(i + c, i + step + c), (i + step + c, i + c)]
        q = product_left_t(jnp.where(is_upper, even3[2], zeros), chain)
        received = lax.ppermute(jnp.where(is_upper, q, chain), "row", pairs)
        if level == 1:
            received, rest = lax.optimization_barrier((received, partner_factors[1:]))
            partner_factors[1:] = rest
        their_s = partner_factors[level - 1]
        own_part = product_left_t(jnp.where(is_lower, their_s, zeros), chain)
        update = product_left_t(even3[1], received) + q
        if level == levels - 1:
            result = lax.cond(
                is_upper,
                lambda c, u, r: c - product(even3[0], u),
                lambda c, u, r: r,
                chain,
                update,
                result,
            )
        else:
            result = jnp.where(is_upper, chain - product(even3[0], update), result)
        chain = jnp.where(is_lower, chain - own_part - received, chain)
    base_out = jnp.where(base == 0, chain, result)

    keep = jnp.where(core == 0, base_out, level0_out)
    give = jnp.where(core == 0, level0_out, base_out)
    got = lax.ppermute(give, "row", swap)
    top = jnp.concatenate([jnp.where(core == 0, keep, got), jnp.where(core == 0, got, keep)], axis=1)
    return jnp.concatenate([top, leafed[width:]], axis=0)


def solution(mesh):
    in_specs = (P("row", "col"), P("row", "col"), P("row", "col"), P("row", "col"), P("row", "col"))
    out_specs = P("row", "col")
    return jax.shard_map(
        on_device, mesh=mesh, in_specs=in_specs, out_specs=out_specs, check_vma=False
    )
```

```python
import jax
import jax.numpy as jnp
from jax import lax
from jax.sharding import PartitionSpec as P


def product(left, right):
    return jnp.dot(left, right, precision=lax.Precision.HIGH, preferred_element_type=jnp.float32)


def product_left_t(left, right):
    return lax.dot_general(
        left,
        right,
        (((0,), (0,)), ((), ())),
        precision=lax.Precision.HIGH,
        preferred_element_type=jnp.float32,
    )


def unit_lower(raw):
    row_ids = lax.broadcasted_iota(jnp.int32, raw.shape, 0)
    col_ids = lax.broadcasted_iota(jnp.int32, raw.shape, 1)
    diagonal = jnp.where(row_ids == col_ids, 1.0, 0.0).astype(raw.dtype)
    return jnp.where(row_ids > col_ids, raw, 0.0) + diagonal


def col_gather(part):
    n_col = lax.axis_size("col")
    me = lax.axis_index("col")
    by_shift = [part]
    for shift in range(1, n_col):
        perm = [(i, (i + shift) % n_col) for i in range(n_col)]
        by_shift.append(lax.ppermute(part, "col", perm))
    stacked = jnp.stack(by_shift)
    blocks = [stacked[(me - b) % n_col] for b in range(n_col)]
    return jnp.concatenate(blocks, axis=1)


def on_device(slab, leaf_v, leaf_t, tree_v, tree_t):
    n_row = lax.axis_size("row")
    levels = n_row.bit_length() - 1
    position = lax.axis_index("row")
    rows = leaf_v.shape[0]
    width = leaf_t.shape[0]

    gathered = col_gather(jnp.concatenate([leaf_v, leaf_t, tree_v, tree_t], axis=0))
    leaf_full = gathered[:rows]
    leaf_tri = gathered[rows:rows + width]
    tree_full = gathered[rows + width:rows + 2 * width]
    tree_tri = gathered[rows + 2 * width:]

    leaf_vectors = unit_lower(leaf_full)
    leaf_factor = jnp.triu(leaf_tri)
    leaf_w = product_left_t(leaf_factor, product_left_t(leaf_vectors, slab))
    leafed = slab - product(leaf_vectors, leaf_w)
    current = leafed[:width]

    tree_vectors = jnp.triu(tree_full)
    tree_factor = jnp.triu(tree_tri)
    tree_joint = product(tree_vectors, tree_factor)
    own3 = jnp.stack([tree_vectors, tree_factor, tree_joint])

    core = position % 2
    base = position - core
    cols = slab.shape[1]
    half = cols // 2
    swap = [(p, p ^ 1) for p in range(n_row)]
    mate3 = lax.ppermute(own3, "row", swap)
    odd3 = jnp.where(core == 1, own3, mate3)
    even3 = jnp.where(core == 0, own3, mate3)

    hw = width // 2
    half_s = jnp.where(core == 0, even3[1][:hw], even3[1][hw:])
    partner_factors = []
    for level in range(1, levels):
        step = 1 << level
        pairs = []
        for i in range(0, n_row, 2 * step):
            pairs += [(i + step, i), (i + step + 1, i + 1)]
        partner_factors.append(lax.ppermute(half_s, "row", pairs))

    is_lower = core == 0
    received = lax.ppermute(current, "row", swap)
    own_h = lax.dynamic_slice(current, (0, core * half), (width, half))
    early = product_left_t(jnp.where(is_lower, odd3[1], odd3[2]), own_h)
    early, received, partner_factors[0] = lax.optimization_barrier((early, received, partner_factors[0]))
    recv_h = lax.dynamic_slice(received, (0, core * half), (width, half))
    update = early + product_left_t(jnp.where(is_lower, odd3[2], odd3[1]), recv_h)
    upper_h = jnp.where(is_lower, recv_h, own_h)
    level0_out = upper_h - product(odd3[0], update)
    chain = jnp.where(is_lower, own_h, recv_h) - update

    zeros = jnp.zeros_like(tree_factor)
    result = chain
    for level in range(1, levels):
        step = 1 << level
        phase = base % (2 * step)
        is_lower = phase == 0
        is_upper = phase == step
        pairs = []
        for i in range(0, n_row, 2 * step):
            for c in range(2):
                pairs += [(i + c, i + step + c), (i + step + c, i + c)]
        q = product_left_t(jnp.where(is_upper, even3[2], zeros), chain)
        received = lax.ppermute(jnp.where(is_upper, q, chain), "row", pairs)
        if level == 1:
            received, rest = lax.optimization_barrier((received, partner_factors[1:]))
            partner_factors[1:] = rest
        mine = partner_factors[level - 1]
        mates = lax.ppermute(mine, "row", swap)
        top_rows = jnp.where(is_lower & (core == 0), mine, jnp.where(is_lower, mates, 0.0))
        bottom_rows = jnp.where(is_lower & (core == 0), mates, jnp.where(is_lower, mine, 0.0))
        own_part = product_left_t(top_rows, chain[:hw]) + product_left_t(bottom_rows, chain[hw:])
        update = product_left_t(even3[1], received) + q
        result = jnp.where(is_upper, chain - product(even3[0], update), result)
        chain = jnp.where(is_lower, chain - own_part - received, chain)
    base_out = jnp.where(base == 0, chain, result)

    keep = jnp.where(core == 0, base_out, level0_out)
    give = jnp.where(core == 0, level0_out, base_out)
    got = lax.ppermute(give, "row", swap)
    top = jnp.concatenate([jnp.where(core == 0, keep, got), jnp.where(core == 0, got, keep)], axis=1)
    return jnp.concatenate([top, leafed[width:]], axis=0)


def solution(mesh):
    in_specs = (P("row", "col"), P("row", "col"), P("row", "col"), P("row", "col"), P("row", "col"))
    out_specs = P("row", "col")
    return jax.shard_map(
        on_device, mesh=mesh, in_specs=in_specs, out_specs=out_specs, check_vma=False
    )
```

```python
import jax
import jax.numpy as jnp
from jax import lax
from jax.sharding import PartitionSpec as P


def product(left, right):
    return jnp.dot(left, right, precision=lax.Precision.HIGH, preferred_element_type=jnp.float32)


def product_left_t(left, right):
    return lax.dot_general(
        left,
        right,
        (((0,), (0,)), ((), ())),
        precision=lax.Precision.HIGH,
        preferred_element_type=jnp.float32,
    )


def unit_lower(raw):
    row_ids = lax.broadcasted_iota(jnp.int32, raw.shape, 0)
    col_ids = lax.broadcasted_iota(jnp.int32, raw.shape, 1)
    diagonal = jnp.where(row_ids == col_ids, 1.0, 0.0).astype(raw.dtype)
    return jnp.where(row_ids > col_ids, raw, 0.0) + diagonal


def col_gather(part):
    n_col = lax.axis_size("col")
    me = lax.axis_index("col")
    by_shift = [part]
    for shift in range(1, n_col):
        perm = [(i, (i + shift) % n_col) for i in range(n_col)]
        by_shift.append(lax.ppermute(part, "col", perm))
    stacked = jnp.stack(by_shift)
    blocks = [stacked[(me - b) % n_col] for b in range(n_col)]
    return jnp.concatenate(blocks, axis=1)


def on_device(slab, leaf_v, leaf_t, tree_v, tree_t):
    n_row = lax.axis_size("row")
    levels = n_row.bit_length() - 1
    position = lax.axis_index("row")
    rows = leaf_v.shape[0]
    width = leaf_t.shape[0]

    gathered = col_gather(jnp.concatenate([leaf_v, leaf_t, tree_v, tree_t], axis=0))
    leaf_full = gathered[:rows]
    leaf_tri = gathered[rows:rows + width]
    tree_full = gathered[rows + width:rows + 2 * width]
    tree_tri = gathered[rows + 2 * width:]

    leaf_vectors = unit_lower(leaf_full)
    leaf_factor = jnp.triu(leaf_tri)
    leaf_w = product_left_t(leaf_factor, product_left_t(leaf_vectors, slab))
    leafed = slab - product(leaf_vectors, leaf_w)
    current = leafed[:width]

    tree_vectors = jnp.triu(tree_full)
    tree_factor = jnp.triu(tree_tri)
    tree_joint = product(tree_vectors, tree_factor)
    own3 = jnp.stack([tree_vectors, tree_factor, tree_joint])

    core = position % 2
    base = position - core
    cols = slab.shape[1]
    half = cols // 2
    swap = [(p, p ^ 1) for p in range(n_row)]
    mate3 = lax.ppermute(own3, "row", swap)
    odd3 = jnp.where(core == 1, own3, mate3)
    even3 = jnp.where(core == 0, own3, mate3)

    hw = width // 2
    half_s = jnp.where(core == 0, even3[1][:hw], even3[1][hw:])
    partner_factors = []
    for level in range(1, levels):
        step = 1 << level
        pairs = []
        for i in range(0, n_row, 2 * step):
            pairs += [(i + step, i), (i + step + 1, i + 1)]
        partner_factors.append(lax.ppermute(half_s, "row", pairs))

    is_lower = core == 0
    received = lax.ppermute(current, "row", swap)
    own_h = lax.dynamic_slice(current, (0, core * half), (width, half))
    early = product_left_t(jnp.where(is_lower, odd3[1], odd3[2]), own_h)
    early, received = lax.optimization_barrier((early, received))
    recv_h = lax.dynamic_slice(received, (0, core * half), (width, half))
    update = early + product_left_t(jnp.where(is_lower, odd3[2], odd3[1]), recv_h)
    upper_h = jnp.where(is_lower, recv_h, own_h)
    level0_out = upper_h - product(odd3[0], update)
    chain = jnp.where(is_lower, own_h, recv_h) - update

    zeros = jnp.zeros_like(tree_factor)
    result = chain
    for level in range(1, levels):
        step = 1 << level
        phase = base % (2 * step)
        is_lower = phase == 0
        is_upper = phase == step
        pairs = []
        for i in range(0, n_row, 2 * step):
            for c in range(2):
                pairs += [(i + c, i + step + c), (i + step + c, i + c)]
        q = product_left_t(jnp.where(is_upper, even3[2], zeros), chain)
        received = lax.ppermute(jnp.where(is_upper, q, chain), "row", pairs)
        received, mine = lax.optimization_barrier((received, partner_factors[level - 1]))
        mates = lax.ppermute(mine, "row", swap)
        top_rows = jnp.where(is_lower & (core == 0), mine, jnp.where(is_lower, mates, 0.0))
        bottom_rows = jnp.where(is_lower & (core == 0), mates, jnp.where(is_lower, mine, 0.0))
        own_part = product_left_t(top_rows, chain[:hw]) + product_left_t(bottom_rows, chain[hw:])
        update = product_left_t(even3[1], received) + q
        result = jnp.where(is_upper, chain - product(even3[0], update), result)
        chain = jnp.where(is_lower, chain - own_part - received, chain)
    base_out = jnp.where(base == 0, chain, result)

    keep = jnp.where(core == 0, base_out, level0_out)
    give = jnp.where(core == 0, level0_out, base_out)
    got = lax.ppermute(give, "row", swap)
    top = jnp.concatenate([jnp.where(core == 0, keep, got), jnp.where(core == 0, got, keep)], axis=1)
    return jnp.concatenate([top, leafed[width:]], axis=0)


def solution(mesh):
    in_specs = (P("row", "col"), P("row", "col"), P("row", "col"), P("row", "col"), P("row", "col"))
    out_specs = P("row", "col")
    return jax.shard_map(
        on_device, mesh=mesh, in_specs=in_specs, out_specs=out_specs, check_vma=False
    )
```

```python
import jax
import jax.numpy as jnp
from jax import lax
from jax.sharding import PartitionSpec as P


def product(left, right):
    return jnp.dot(left, right, precision=lax.Precision.HIGH, preferred_element_type=jnp.float32)


def product_left_t(left, right):
    return lax.dot_general(
        left,
        right,
        (((0,), (0,)), ((), ())),
        precision=lax.Precision.HIGH,
        preferred_element_type=jnp.float32,
    )


def unit_lower(raw):
    row_ids = lax.broadcasted_iota(jnp.int32, raw.shape, 0)
    col_ids = lax.broadcasted_iota(jnp.int32, raw.shape, 1)
    diagonal = jnp.where(row_ids == col_ids, 1.0, 0.0).astype(raw.dtype)
    return jnp.where(row_ids > col_ids, raw, 0.0) + diagonal


def col_gather(part):
    n_col = lax.axis_size("col")
    me = lax.axis_index("col")
    by_shift = [part]
    for shift in range(1, n_col):
        perm = [(i, (i + shift) % n_col) for i in range(n_col)]
        by_shift.append(lax.ppermute(part, "col", perm))
    stacked = jnp.stack(by_shift)
    blocks = [stacked[(me - b) % n_col] for b in range(n_col)]
    return jnp.concatenate(blocks, axis=1)


def on_device(slab, leaf_v, leaf_t, tree_v, tree_t):
    n_row = lax.axis_size("row")
    levels = n_row.bit_length() - 1
    position = lax.axis_index("row")
    rows = leaf_v.shape[0]
    width = leaf_t.shape[0]

    leaf_full = col_gather(leaf_v)
    leaf_tri = col_gather(leaf_t)
    tree_full = col_gather(tree_v)
    tree_tri = col_gather(tree_t)

    leaf_vectors = unit_lower(leaf_full)
    leaf_factor = jnp.triu(leaf_tri)
    leaf_w = product_left_t(leaf_factor, product_left_t(leaf_vectors, slab))
    leafed = slab - product(leaf_vectors, leaf_w)
    current = leafed[:width]

    tree_vectors = jnp.triu(tree_full)
    tree_factor = jnp.triu(tree_tri)
    tree_joint = product(tree_vectors, tree_factor)
    own3 = jnp.stack([tree_vectors, tree_factor, tree_joint])

    core = position % 2
    base = position - core
    cols = slab.shape[1]
    half = cols // 2
    swap = [(p, p ^ 1) for p in range(n_row)]
    mate3 = lax.ppermute(own3, "row", swap)
    odd3 = jnp.where(core == 1, own3, mate3)
    even3 = jnp.where(core == 0, own3, mate3)

    hw = width // 2
    half_s = jnp.where(core == 0, even3[1][:hw], even3[1][hw:])
    partner_factors = []
    for level in range(1, levels):
        step = 1 << level
        pairs = []
        for i in range(0, n_row, 2 * step):
            pairs += [(i + step, i), (i + step + 1, i + 1)]
        partner_factors.append(lax.ppermute(half_s, "row", pairs))

    is_lower = core == 0
    received = lax.ppermute(current, "row", swap)
    own_h = lax.dynamic_slice(current, (0, core * half), (width, half))
    early = product_left_t(jnp.where(is_lower, odd3[1], odd3[2]), own_h)
    early, received, partner_factors[0] = lax.optimization_barrier((early, received, partner_factors[0]))
    recv_h = lax.dynamic_slice(received, (0, core * half), (width, half))
    update = early + product_left_t(jnp.where(is_lower, odd3[2], odd3[1]), recv_h)
    upper_h = jnp.where(is_lower, recv_h, own_h)
    level0_out = upper_h - product(odd3[0], update)
    chain = jnp.where(is_lower, own_h, recv_h) - update

    zeros = jnp.zeros_like(tree_factor)
    result = chain
    for level in range(1, levels):
        step = 1 << level
        phase = base % (2 * step)
        is_lower = phase == 0
        is_upper = phase == step
        pairs = []
        for i in range(0, n_row, 2 * step):
            for c in range(2):
                pairs += [(i + c, i + step + c), (i + step + c, i + c)]
        q = product_left_t(jnp.where(is_upper, even3[2], zeros), chain)
        received = lax.ppermute(jnp.where(is_upper, q, chain), "row", pairs)
        if level == 1:
            received, rest = lax.optimization_barrier((received, partner_factors[1:]))
            partner_factors[1:] = rest
        mine = partner_factors[level - 1]
        mates = lax.ppermute(mine, "row", swap)
        top_rows = jnp.where(is_lower & (core == 0), mine, jnp.where(is_lower, mates, 0.0))
        bottom_rows = jnp.where(is_lower & (core == 0), mates, jnp.where(is_lower, mine, 0.0))
        own_part = product_left_t(top_rows, chain[:hw]) + product_left_t(bottom_rows, chain[hw:])
        update = product_left_t(even3[1], received) + q
        result = jnp.where(is_upper, chain - product(even3[0], update), result)
        chain = jnp.where(is_lower, chain - own_part - received, chain)
    base_out = jnp.where(base == 0, chain, result)

    keep = jnp.where(core == 0, base_out, level0_out)
    give = jnp.where(core == 0, level0_out, base_out)
    got = lax.ppermute(give, "row", swap)
    top = jnp.concatenate([jnp.where(core == 0, keep, got), jnp.where(core == 0, got, keep)], axis=1)
    return jnp.concatenate([top, leafed[width:]], axis=0)


def solution(mesh):
    in_specs = (P("row", "col"), P("row", "col"), P("row", "col"), P("row", "col"), P("row", "col"))
    out_specs = P("row", "col")
    return jax.shard_map(
        on_device, mesh=mesh, in_specs=in_specs, out_specs=out_specs, check_vma=False
    )
```

```python
import jax
import jax.numpy as jnp
from jax import lax
from jax.sharding import PartitionSpec as P


def product(left, right):
    return jnp.dot(left, right, precision=lax.Precision.HIGH, preferred_element_type=jnp.float32)


def product_left_t(left, right):
    return lax.dot_general(
        left,
        right,
        (((0,), (0,)), ((), ())),
        precision=lax.Precision.HIGH,
        preferred_element_type=jnp.float32,
    )


def unit_lower(raw):
    row_ids = lax.broadcasted_iota(jnp.int32, raw.shape, 0)
    col_ids = lax.broadcasted_iota(jnp.int32, raw.shape, 1)
    diagonal = jnp.where(row_ids == col_ids, 1.0, 0.0).astype(raw.dtype)
    return jnp.where(row_ids > col_ids, raw, 0.0) + diagonal


def col_gather(part):
    n_col = lax.axis_size("col")
    me = lax.axis_index("col")
    by_shift = [part]
    for shift in range(1, n_col):
        perm = [(i, (i + shift) % n_col) for i in range(n_col)]
        by_shift.append(lax.ppermute(part, "col", perm))
    stacked = jnp.stack(by_shift)
    blocks = [stacked[(me - b) % n_col] for b in range(n_col)]
    return jnp.concatenate(blocks, axis=1)


def on_device(slab, leaf_v, leaf_t, tree_v, tree_t):
    n_row = lax.axis_size("row")
    levels = n_row.bit_length() - 1
    position = lax.axis_index("row")
    rows = leaf_v.shape[0]
    width = leaf_t.shape[0]

    leaf_full = col_gather(leaf_v)
    leaf_tri = col_gather(leaf_t)
    tree_full = col_gather(tree_v)
    tree_tri = col_gather(tree_t)

    leaf_vectors = unit_lower(leaf_full)
    leaf_factor = jnp.triu(leaf_tri)
    leaf_w = product_left_t(leaf_factor, product_left_t(leaf_vectors, slab))
    leafed = slab - product(leaf_vectors, leaf_w)
    current = leafed[:width]

    tree_vectors = jnp.triu(tree_full)
    tree_factor = jnp.triu(tree_tri)
    tree_joint = product(tree_vectors, tree_factor)
    own3 = jnp.stack([tree_vectors, tree_factor, tree_joint])

    core = position % 2
    base = position - core
    cols = slab.shape[1]
    half = cols // 2
    swap = [(p, p ^ 1) for p in range(n_row)]
    mate3 = lax.ppermute(own3, "row", swap)
    odd3 = jnp.where(core == 1, own3, mate3)
    even3 = jnp.where(core == 0, own3, mate3)

    hw = width // 2
    half_s = jnp.where(core == 0, even3[1][:hw], even3[1][hw:])
    partner_factors = []
    for level in range(1, levels):
        step = 1 << level
        pairs = []
        for i in range(0, n_row, 2 * step):
            pairs += [(i + step, i), (i + step + 1, i + 1)]
        partner_factors.append(lax.ppermute(half_s, "row", pairs))

    is_lower = core == 0
    received = lax.ppermute(current, "row", swap)
    own_h = lax.dynamic_slice(current, (0, core * half), (width, half))
    early = product_left_t(jnp.where(is_lower, odd3[1], odd3[2]), own_h)
    early, received, partner_factors[0] = lax.optimization_barrier((early, received, partner_factors[0]))
    recv_h = lax.dynamic_slice(received, (0, core * half), (width, half))
    update = early + product_left_t(jnp.where(is_lower, odd3[2], odd3[1]), recv_h)
    upper_h = jnp.where(is_lower, recv_h, own_h)
    level0_out = upper_h - product(odd3[0], update)
    chain = jnp.where(is_lower, own_h, recv_h) - update

    zeros = jnp.zeros_like(tree_factor)
    result = chain
    for level in range(1, levels):
        step = 1 << level
        phase = base % (2 * step)
        is_lower = phase == 0
        is_upper = phase == step
        pairs = []
        for i in range(0, n_row, 2 * step):
            for c in range(2):
                pairs += [(i + c, i + step + c), (i + step + c, i + c)]
        q = product_left_t(jnp.where(is_upper, even3[2], zeros), chain)
        received = lax.ppermute(jnp.where(is_upper, q, chain), "row", pairs)
        if level == 1:
            received, rest = lax.optimization_barrier((received, partner_factors[1:]))
            partner_factors[1:] = rest
        mine = partner_factors[level - 1]
        mates = lax.ppermute(mine, "row", swap)
        top_rows = jnp.where(is_lower & (core == 0), mine, jnp.where(is_lower, mates, 0.0))
        bottom_rows = jnp.where(is_lower & (core == 0), mates, jnp.where(is_lower, mine, 0.0))
        own_part = product_left_t(top_rows, chain[:hw]) + product_left_t(bottom_rows, chain[hw:])
        own_part, received = lax.optimization_barrier((own_part, received))
        update = product_left_t(even3[1], received) + q
        result = jnp.where(is_upper, chain - product(even3[0], update), result)
        chain = jnp.where(is_lower, chain - own_part - received, chain)
    base_out = jnp.where(base == 0, chain, result)

    keep = jnp.where(core == 0, base_out, level0_out)
    give = jnp.where(core == 0, level0_out, base_out)
    got = lax.ppermute(give, "row", swap)
    top = jnp.concatenate([jnp.where(core == 0, keep, got), jnp.where(core == 0, got, keep)], axis=1)
    return jnp.concatenate([top, leafed[width:]], axis=0)


def solution(mesh):
    in_specs = (P("row", "col"), P("row", "col"), P("row", "col"), P("row", "col"), P("row", "col"))
    out_specs = P("row", "col")
    return jax.shard_map(
        on_device, mesh=mesh, in_specs=in_specs, out_specs=out_specs, check_vma=False
    )
```

```python
import jax
import jax.numpy as jnp
from jax import lax
from jax.sharding import PartitionSpec as P


def product(left, right):
    return jnp.dot(left, right, precision=lax.Precision.HIGH, preferred_element_type=jnp.float32)


def product_left_t(left, right):
    return lax.dot_general(
        left,
        right,
        (((0,), (0,)), ((), ())),
        precision=lax.Precision.HIGH,
        preferred_element_type=jnp.float32,
    )


def unit_lower(raw):
    row_ids = lax.broadcasted_iota(jnp.int32, raw.shape, 0)
    col_ids = lax.broadcasted_iota(jnp.int32, raw.shape, 1)
    diagonal = jnp.where(row_ids == col_ids, 1.0, 0.0).astype(raw.dtype)
    return jnp.where(row_ids > col_ids, raw, 0.0) + diagonal


def col_gather(part):
    n_col = lax.axis_size("col")
    me = lax.axis_index("col")
    by_shift = [part]
    for shift in range(1, n_col):
        perm = [(i, (i + shift) % n_col) for i in range(n_col)]
        by_shift.append(lax.ppermute(part, "col", perm))
    stacked = jnp.stack(by_shift)
    blocks = [stacked[(me - b) % n_col] for b in range(n_col)]
    return jnp.concatenate(blocks, axis=1)


def on_device(slab, leaf_v, leaf_t, tree_v, tree_t):
    n_row = lax.axis_size("row")
    levels = n_row.bit_length() - 1
    position = lax.axis_index("row")
    rows = leaf_v.shape[0]
    width = leaf_t.shape[0]

    leaf_full = col_gather(leaf_v)
    leaf_tri = col_gather(leaf_t)
    tree_full = col_gather(tree_v)
    tree_tri = col_gather(tree_t)

    tree_vectors = jnp.triu(tree_full)
    tree_factor = jnp.triu(tree_tri)
    tree_joint = product(tree_vectors, tree_factor)
    own3 = jnp.stack([tree_vectors, tree_factor, tree_joint])

    core = position % 2
    base = position - core
    cols = slab.shape[1]
    half = cols // 2
    swap = [(p, p ^ 1) for p in range(n_row)]
    mate3 = lax.ppermute(own3, "row", swap)
    odd3 = jnp.where(core == 1, own3, mate3)
    even3 = jnp.where(core == 0, own3, mate3)

    hw = width // 2
    mate_s = lax.ppermute(tree_factor[hw:], "row", swap)
    half_s = jnp.where(core == 0, tree_factor[:hw], mate_s)
    partner_factors = []
    for level in range(1, levels):
        step = 1 << level
        pairs = []
        for i in range(0, n_row, 2 * step):
            pairs += [(i + step, i), (i + step + 1, i + 1)]
        partner_factors.append(lax.ppermute(half_s, "row", pairs))

    leaf_full, leaf_tri, partner_factors[0] = lax.optimization_barrier((leaf_full, leaf_tri, partner_factors[0]))
    leaf_vectors = unit_lower(leaf_full)
    leaf_factor = jnp.triu(leaf_tri)
    leaf_w = product_left_t(leaf_factor, product_left_t(leaf_vectors, slab))
    leafed = slab - product(leaf_vectors, leaf_w)
    current = leafed[:width]

    is_lower = core == 0
    received = lax.ppermute(current, "row", swap)
    own_h = lax.dynamic_slice(current, (0, core * half), (width, half))
    early = product_left_t(jnp.where(is_lower, odd3[1], odd3[2]), own_h)
    early, received = lax.optimization_barrier((early, received))
    recv_h = lax.dynamic_slice(received, (0, core * half), (width, half))
    update = early + product_left_t(jnp.where(is_lower, odd3[2], odd3[1]), recv_h)
    upper_h = jnp.where(is_lower, recv_h, own_h)
    level0_out = upper_h - product(odd3[0], update)
    chain = jnp.where(is_lower, own_h, recv_h) - update

    zeros = jnp.zeros_like(tree_factor)
    result = chain
    for level in range(1, levels):
        step = 1 << level
        phase = base % (2 * step)
        is_lower = phase == 0
        is_upper = phase == step
        pairs = []
        for i in range(0, n_row, 2 * step):
            for c in range(2):
                pairs += [(i + c, i + step + c), (i + step + c, i + c)]
        q = product_left_t(jnp.where(is_upper, even3[2], zeros), chain)
        received = lax.ppermute(jnp.where(is_upper, q, chain), "row", pairs)
        if level == 1:
            received, rest = lax.optimization_barrier((received, partner_factors[1:]))
            partner_factors[1:] = rest
        mine = partner_factors[level - 1]
        mates = lax.ppermute(mine, "row", swap)
        top_rows = jnp.where(is_lower & (core == 0), mine, jnp.where(is_lower, mates, 0.0))
        bottom_rows = jnp.where(is_lower & (core == 0), mates, jnp.where(is_lower, mine, 0.0))
        own_part = product_left_t(top_rows, chain[:hw]) + product_left_t(bottom_rows, chain[hw:])
        own_part, received = lax.optimization_barrier((own_part, received))
        update = product_left_t(even3[1], received) + q
        result = jnp.where(is_upper, chain - product(even3[0], update), result)
        chain = jnp.where(is_lower, chain - own_part - received, chain)
    base_out = jnp.where(base == 0, chain, result)

    keep = jnp.where(core == 0, base_out, level0_out)
    give = jnp.where(core == 0, level0_out, base_out)
    got = lax.ppermute(give, "row", swap)
    top = jnp.concatenate([jnp.where(core == 0, keep, got), jnp.where(core == 0, got, keep)], axis=1)
    return jnp.concatenate([top, leafed[width:]], axis=0)


def solution(mesh):
    in_specs = (P("row", "col"), P("row", "col"), P("row", "col"), P("row", "col"), P("row", "col"))
    out_specs = P("row", "col")
    return jax.shard_map(
        on_device, mesh=mesh, in_specs=in_specs, out_specs=out_specs, check_vma=False
    )
```

```python
import jax
import jax.numpy as jnp
from jax import lax
from jax.sharding import PartitionSpec as P


def product(left, right):
    return jnp.dot(left, right, precision=lax.Precision.HIGH, preferred_element_type=jnp.float32)


def product_left_t(left, right):
    return lax.dot_general(
        left,
        right,
        (((0,), (0,)), ((), ())),
        precision=lax.Precision.HIGH,
        preferred_element_type=jnp.float32,
    )


def unit_lower(raw):
    row_ids = lax.broadcasted_iota(jnp.int32, raw.shape, 0)
    col_ids = lax.broadcasted_iota(jnp.int32, raw.shape, 1)
    diagonal = jnp.where(row_ids == col_ids, 1.0, 0.0).astype(raw.dtype)
    return jnp.where(row_ids > col_ids, raw, 0.0) + diagonal


def col_gather(part):
    n_col = lax.axis_size("col")
    me = lax.axis_index("col")
    by_shift = [part]
    for shift in range(1, n_col):
        perm = [(i, (i + shift) % n_col) for i in range(n_col)]
        by_shift.append(lax.ppermute(part, "col", perm))
    stacked = jnp.stack(by_shift)
    blocks = [stacked[(me - b) % n_col] for b in range(n_col)]
    return jnp.concatenate(blocks, axis=1)


def on_device(slab, leaf_v, leaf_t, tree_v, tree_t):
    n_row = lax.axis_size("row")
    levels = n_row.bit_length() - 1
    position = lax.axis_index("row")
    rows = leaf_v.shape[0]
    width = leaf_t.shape[0]

    leaf_full = col_gather(leaf_v)
    leaf_tri = col_gather(leaf_t)
    tree_full = col_gather(tree_v)
    tree_tri = col_gather(tree_t)

    tree_vectors = jnp.triu(tree_full)
    tree_factor = jnp.triu(tree_tri)
    tree_joint = product(tree_vectors, tree_factor)
    own3 = jnp.stack([tree_vectors, tree_factor, tree_joint])

    core = position % 2
    base = position - core
    cols = slab.shape[1]
    half = cols // 2
    swap = [(p, p ^ 1) for p in range(n_row)]
    mate3 = lax.ppermute(own3, "row", swap)
    odd3 = jnp.where(core == 1, own3, mate3)
    even3 = jnp.where(core == 0, own3, mate3)

    hw = width // 2
    mate_s = lax.ppermute(tree_factor[hw:], "row", swap)
    half_s = jnp.where(core == 0, tree_factor[:hw], mate_s)
    partner_factors = []
    for level in range(1, levels):
        step = 1 << level
        pairs = []
        for i in range(0, n_row, 2 * step):
            pairs += [(i + step, i), (i + step + 1, i + 1)]
        partner_factors.append(lax.ppermute(half_s, "row", pairs))

    leaf_full, leaf_tri, partner_factors[0] = lax.optimization_barrier((leaf_full, leaf_tri, partner_factors[0]))
    leaf_vectors = unit_lower(leaf_full)
    leaf_factor = jnp.triu(leaf_tri)
    leaf_w = product_left_t(leaf_factor, product_left_t(leaf_vectors, slab))
    leafed = slab - product(leaf_vectors, leaf_w)
    current = leafed[:width]

    is_lower = core == 0
    received = lax.ppermute(current, "row", swap)
    own_h = lax.dynamic_slice(current, (0, core * half), (width, half))
    early = product_left_t(jnp.where(is_lower, odd3[1], odd3[2]), own_h)
    early, received = lax.optimization_barrier((early, received))
    recv_h = lax.dynamic_slice(received, (0, core * half), (width, half))
    update = early + product_left_t(jnp.where(is_lower, odd3[2], odd3[1]), recv_h)
    upper_h = jnp.where(is_lower, recv_h, own_h)
    level0_out = upper_h - product(odd3[0], update)
    chain = jnp.where(is_lower, own_h, recv_h) - update

    zeros = jnp.zeros_like(tree_factor)
    result = chain
    for level in range(1, levels):
        step = 1 << level
        phase = base % (2 * step)
        is_lower = phase == 0
        is_upper = phase == step
        pairs = []
        for i in range(0, n_row, 2 * step):
            for c in range(2):
                pairs += [(i + c, i + step + c), (i + step + c, i + c)]
        q = product_left_t(jnp.where(is_upper, even3[2], zeros), chain)
        received = lax.ppermute(jnp.where(is_upper, q, chain), "row", pairs)
        if level == 1:
            mates_of = [lax.ppermute(partner_factors[0], "row", swap)]
            received, rest = lax.optimization_barrier((received, partner_factors[1:]))
            partner_factors[1:] = rest
            if rest:
                swapped_rest = lax.ppermute(jnp.stack(rest), "row", swap)
                mates_of += [swapped_rest[k] for k in range(len(rest))]
        mine = partner_factors[level - 1]
        mates = mates_of[level - 1]
        top_rows = jnp.where(is_lower & (core == 0), mine, jnp.where(is_lower, mates, 0.0))
        bottom_rows = jnp.where(is_lower & (core == 0), mates, jnp.where(is_lower, mine, 0.0))
        own_part = product_left_t(top_rows, chain[:hw]) + product_left_t(bottom_rows, chain[hw:])
        own_part, received = lax.optimization_barrier((own_part, received))
        update = product_left_t(even3[1], received) + q
        result = jnp.where(is_upper, chain - product(even3[0], update), result)
        chain = jnp.where(is_lower, chain - own_part - received, chain)
    base_out = jnp.where(base == 0, chain, result)

    keep = jnp.where(core == 0, base_out, level0_out)
    give = jnp.where(core == 0, level0_out, base_out)
    got = lax.ppermute(give, "row", swap)
    top = jnp.concatenate([jnp.where(core == 0, keep, got), jnp.where(core == 0, got, keep)], axis=1)
    return jnp.concatenate([top, leafed[width:]], axis=0)


def solution(mesh):
    in_specs = (P("row", "col"), P("row", "col"), P("row", "col"), P("row", "col"), P("row", "col"))
    out_specs = P("row", "col")
    return jax.shard_map(
        on_device, mesh=mesh, in_specs=in_specs, out_specs=out_specs, check_vma=False
    )
```

```python
import jax
import jax.numpy as jnp
from jax import lax
from jax.sharding import PartitionSpec as P


def product(left, right):
    return jnp.dot(left, right, precision=lax.Precision.HIGH, preferred_element_type=jnp.float32)


def product_left_t(left, right):
    return lax.dot_general(
        left,
        right,
        (((0,), (0,)), ((), ())),
        precision=lax.Precision.HIGH,
        preferred_element_type=jnp.float32,
    )


def unit_lower(raw):
    row_ids = lax.broadcasted_iota(jnp.int32, raw.shape, 0)
    col_ids = lax.broadcasted_iota(jnp.int32, raw.shape, 1)
    diagonal = jnp.where(row_ids == col_ids, 1.0, 0.0).astype(raw.dtype)
    return jnp.where(row_ids > col_ids, raw, 0.0) + diagonal


def col_gather(part):
    n_col = lax.axis_size("col")
    me = lax.axis_index("col")
    by_shift = [part]
    for shift in range(1, n_col):
        perm = [(i, (i + shift) % n_col) for i in range(n_col)]
        by_shift.append(lax.ppermute(part, "col", perm))
    stacked = jnp.stack(by_shift)
    blocks = [stacked[(me - b) % n_col] for b in range(n_col)]
    return jnp.concatenate(blocks, axis=1)


def on_device(slab, leaf_v, leaf_t, tree_v, tree_t):
    n_row = lax.axis_size("row")
    levels = n_row.bit_length() - 1
    position = lax.axis_index("row")
    rows = leaf_v.shape[0]
    width = leaf_t.shape[0]

    leaf_full = col_gather(leaf_v)
    leaf_tri = col_gather(leaf_t)
    tree_full = col_gather(tree_v)
    tree_tri = col_gather(tree_t)

    tree_vectors = jnp.triu(tree_full)
    tree_factor = jnp.triu(tree_tri)
    tree_joint = product(tree_vectors, tree_factor)
    own3 = jnp.stack([tree_vectors, tree_factor, tree_joint])

    core = position % 2
    base = position - core
    cols = slab.shape[1]
    half = cols // 2
    swap = [(p, p ^ 1) for p in range(n_row)]
    mate3 = lax.ppermute(own3, "row", swap)
    odd3 = jnp.where(core == 1, own3, mate3)
    even3 = jnp.where(core == 0, own3, mate3)

    hw = width // 2
    mate_s = lax.ppermute(tree_factor[hw:], "row", swap)
    half_s = jnp.where(core == 0, tree_factor[:hw], mate_s)
    partner_factors = []
    for level in range(1, levels):
        step = 1 << level
        pairs = []
        for i in range(0, n_row, 2 * step):
            pairs += [(i + step, i), (i + step + 1, i + 1)]
        partner_factors.append(lax.ppermute(half_s, "row", pairs))

    leaf_full, leaf_tri, partner_factors = lax.optimization_barrier((leaf_full, leaf_tri, partner_factors))
    leaf_vectors = unit_lower(leaf_full)
    leaf_factor = jnp.triu(leaf_tri)
    leaf_w = product_left_t(leaf_factor, product_left_t(leaf_vectors, slab))
    leafed = slab - product(leaf_vectors, leaf_w)
    current = leafed[:width]

    is_lower = core == 0
    received = lax.ppermute(current, "row", swap)
    own_h = lax.dynamic_slice(current, (0, core * half), (width, half))
    early = product_left_t(jnp.where(is_lower, odd3[1], odd3[2]), own_h)
    early, received = lax.optimization_barrier((early, received))
    recv_h = lax.dynamic_slice(received, (0, core * half), (width, half))
    update = early + product_left_t(jnp.where(is_lower, odd3[2], odd3[1]), recv_h)
    upper_h = jnp.where(is_lower, recv_h, own_h)
    level0_out = upper_h - product(odd3[0], update)
    chain = jnp.where(is_lower, own_h, recv_h) - update

    zeros = jnp.zeros_like(tree_factor)
    result = chain
    for level in range(1, levels):
        step = 1 << level
        phase = base % (2 * step)
        is_lower = phase == 0
        is_upper = phase == step
        pairs = []
        for i in range(0, n_row, 2 * step):
            for c in range(2):
                pairs += [(i + c, i + step + c), (i + step + c, i + c)]
        q = product_left_t(jnp.where(is_upper, even3[2], zeros), chain)
        received = lax.ppermute(jnp.where(is_upper, q, chain), "row", pairs)
        mine = partner_factors[level - 1]
        mates = lax.ppermute(mine, "row", swap)
        top_rows = jnp.where(is_lower & (core == 0), mine, jnp.where(is_lower, mates, 0.0))
        bottom_rows = jnp.where(is_lower & (core == 0), mates, jnp.where(is_lower, mine, 0.0))
        own_part = product_left_t(top_rows, chain[:hw]) + product_left_t(bottom_rows, chain[hw:])
        own_part, received = lax.optimization_barrier((own_part, received))
        update = product_left_t(even3[1], received) + q
        result = jnp.where(is_upper, chain - product(even3[0], update), result)
        chain = jnp.where(is_lower, chain - own_part - received, chain)
    base_out = jnp.where(base == 0, chain, result)

    keep = jnp.where(core == 0, base_out, level0_out)
    give = jnp.where(core == 0, level0_out, base_out)
    got = lax.ppermute(give, "row", swap)
    top = jnp.concatenate([jnp.where(core == 0, keep, got), jnp.where(core == 0, got, keep)], axis=1)
    return jnp.concatenate([top, leafed[width:]], axis=0)


def solution(mesh):
    in_specs = (P("row", "col"), P("row", "col"), P("row", "col"), P("row", "col"), P("row", "col"))
    out_specs = P("row", "col")
    return jax.shard_map(
        on_device, mesh=mesh, in_specs=in_specs, out_specs=out_specs, check_vma=False
    )
```

```python
import jax
import jax.numpy as jnp
from jax import lax
from jax.sharding import PartitionSpec as P


def product(left, right):
    return jnp.dot(left, right, precision=lax.Precision.HIGH, preferred_element_type=jnp.float32)


def product_left_t(left, right):
    return lax.dot_general(
        left,
        right,
        (((0,), (0,)), ((), ())),
        precision=lax.Precision.HIGH,
        preferred_element_type=jnp.float32,
    )


def unit_lower(raw):
    row_ids = lax.broadcasted_iota(jnp.int32, raw.shape, 0)
    col_ids = lax.broadcasted_iota(jnp.int32, raw.shape, 1)
    diagonal = jnp.where(row_ids == col_ids, 1.0, 0.0).astype(raw.dtype)
    return jnp.where(row_ids > col_ids, raw, 0.0) + diagonal


def col_gather(part):
    n_col = lax.axis_size("col")
    me = lax.axis_index("col")
    by_shift = [part]
    for shift in range(1, n_col):
        perm = [(i, (i + shift) % n_col) for i in range(n_col)]
        by_shift.append(lax.ppermute(part, "col", perm))
    stacked = jnp.stack(by_shift)
    blocks = [stacked[(me - b) % n_col] for b in range(n_col)]
    return jnp.concatenate(blocks, axis=1)


def on_device(slab, leaf_v, leaf_t, tree_v, tree_t):
    n_row = lax.axis_size("row")
    levels = n_row.bit_length() - 1
    position = lax.axis_index("row")
    rows = leaf_v.shape[0]
    width = leaf_t.shape[0]

    leaf_full = col_gather(leaf_v)
    leaf_tri = col_gather(leaf_t)
    tree_full = col_gather(tree_v)
    tree_tri = col_gather(tree_t)

    tree_vectors = jnp.triu(tree_full)
    tree_factor = jnp.triu(tree_tri)
    tree_joint = product(tree_vectors, tree_factor)
    own3 = jnp.stack([tree_vectors, tree_factor, tree_joint])

    core = position % 2
    base = position - core
    cols = slab.shape[1]
    half = cols // 2
    swap = [(p, p ^ 1) for p in range(n_row)]
    mate3 = lax.ppermute(own3, "row", swap)
    odd3 = jnp.where(core == 1, own3, mate3)
    even3 = jnp.where(core == 0, own3, mate3)

    hw = width // 2
    partner_factors = []
    for level in range(1, levels):
        step = 1 << level
        to_even = [(i + step, i) for i in range(0, n_row, 2 * step)]
        to_odd = [(i + step, i + 1) for i in range(0, n_row, 2 * step)]
        top_half = lax.ppermute(tree_factor[:hw], "row", to_even)
        bottom_half = lax.ppermute(tree_factor[hw:], "row", to_odd)
        partner_factors.append(jnp.where(core == 0, top_half, bottom_half))

    leaf_full, leaf_tri, partner_factors = lax.optimization_barrier((leaf_full, leaf_tri, partner_factors))
    leaf_vectors = unit_lower(leaf_full)
    leaf_factor = jnp.triu(leaf_tri)
    leaf_w = product_left_t(leaf_factor, product_left_t(leaf_vectors, slab))
    leafed = slab - product(leaf_vectors, leaf_w)
    current = leafed[:width]

    is_lower = core == 0
    received = lax.ppermute(current, "row", swap)
    own_h = lax.dynamic_slice(current, (0, core * half), (width, half))
    early = product_left_t(jnp.where(is_lower, odd3[1], odd3[2]), own_h)
    early, received = lax.optimization_barrier((early, received))
    recv_h = lax.dynamic_slice(received, (0, core * half), (width, half))
    update = early + product_left_t(jnp.where(is_lower, odd3[2], odd3[1]), recv_h)
    upper_h = jnp.where(is_lower, recv_h, own_h)
    level0_out = upper_h - product(odd3[0], update)
    chain = jnp.where(is_lower, own_h, recv_h) - update

    zeros = jnp.zeros_like(tree_factor)
    result = chain
    for level in range(1, levels):
        step = 1 << level
        phase = base % (2 * step)
        is_lower = phase == 0
        is_upper = phase == step
        pairs = []
        for i in range(0, n_row, 2 * step):
            for c in range(2):
                pairs += [(i + c, i + step + c), (i + step + c, i + c)]
        q = product_left_t(jnp.where(is_upper, even3[2], zeros), chain)
        received = lax.ppermute(jnp.where(is_upper, q, chain), "row", pairs)
        mine = partner_factors[level - 1]
        mates = lax.ppermute(mine, "row", swap)
        top_rows = jnp.where(is_lower & (core == 0), mine, jnp.where(is_lower, mates, 0.0))
        bottom_rows = jnp.where(is_lower & (core == 0), mates, jnp.where(is_lower, mine, 0.0))
        own_part = product_left_t(top_rows, chain[:hw]) + product_left_t(bottom_rows, chain[hw:])
        own_part, received = lax.optimization_barrier((own_part, received))
        update = product_left_t(even3[1], received) + q
        result = jnp.where(is_upper, chain - product(even3[0], update), result)
        chain = jnp.where(is_lower, chain - own_part - received, chain)
    base_out = jnp.where(base == 0, chain, result)

    keep = jnp.where(core == 0, base_out, level0_out)
    give = jnp.where(core == 0, level0_out, base_out)
    got = lax.ppermute(give, "row", swap)
    top = jnp.concatenate([jnp.where(core == 0, keep, got), jnp.where(core == 0, got, keep)], axis=1)
    return jnp.concatenate([top, leafed[width:]], axis=0)


def solution(mesh):
    in_specs = (P("row", "col"), P("row", "col"), P("row", "col"), P("row", "col"), P("row", "col"))
    out_specs = P("row", "col")
    return jax.shard_map(
        on_device, mesh=mesh, in_specs=in_specs, out_specs=out_specs, check_vma=False
    )
```

```python
import jax
import jax.numpy as jnp
from jax import lax
from jax.sharding import PartitionSpec as P


def product(left, right):
    return jnp.dot(left, right, precision=lax.Precision.HIGH, preferred_element_type=jnp.float32)


def product_left_t(left, right):
    return lax.dot_general(
        left,
        right,
        (((0,), (0,)), ((), ())),
        precision=lax.Precision.HIGH,
        preferred_element_type=jnp.float32,
    )


def unit_lower(raw):
    row_ids = lax.broadcasted_iota(jnp.int32, raw.shape, 0)
    col_ids = lax.broadcasted_iota(jnp.int32, raw.shape, 1)
    diagonal = jnp.where(row_ids == col_ids, 1.0, 0.0).astype(raw.dtype)
    return jnp.where(row_ids > col_ids, raw, 0.0) + diagonal


def col_gather(part):
    n_col = lax.axis_size("col")
    me = lax.axis_index("col")
    by_shift = [part]
    for shift in range(1, n_col):
        perm = [(i, (i + shift) % n_col) for i in range(n_col)]
        by_shift.append(lax.ppermute(part, "col", perm))
    stacked = jnp.stack(by_shift)
    blocks = [stacked[(me - b) % n_col] for b in range(n_col)]
    return jnp.concatenate(blocks, axis=1)


def on_device(slab, leaf_v, leaf_t, tree_v, tree_t):
    n_row = lax.axis_size("row")
    levels = n_row.bit_length() - 1
    position = lax.axis_index("row")
    rows = leaf_v.shape[0]
    width = leaf_t.shape[0]

    tree_tri = col_gather(tree_t)
    tree_tri, leaf_v, leaf_t, tree_v = lax.optimization_barrier((tree_tri, leaf_v, leaf_t, tree_v))
    leaf_full = col_gather(leaf_v)
    leaf_tri = col_gather(leaf_t)
    tree_full = col_gather(tree_v)

    tree_vectors = jnp.triu(tree_full)
    tree_factor = jnp.triu(tree_tri)
    tree_joint = product(tree_vectors, tree_factor)
    own3 = jnp.stack([tree_vectors, tree_factor, tree_joint])

    core = position % 2
    base = position - core
    cols = slab.shape[1]
    half = cols // 2
    swap = [(p, p ^ 1) for p in range(n_row)]
    mate3 = lax.ppermute(own3, "row", swap)
    odd3 = jnp.where(core == 1, own3, mate3)
    even3 = jnp.where(core == 0, own3, mate3)

    hw = width // 2
    mate_s = lax.ppermute(tree_factor[hw:], "row", swap)
    half_s = jnp.where(core == 0, tree_factor[:hw], mate_s)
    partner_factors = []
    for level in range(1, levels):
        step = 1 << level
        pairs = []
        for i in range(0, n_row, 2 * step):
            pairs += [(i + step, i), (i + step + 1, i + 1)]
        partner_factors.append(lax.ppermute(half_s, "row", pairs))

    leaf_full, leaf_tri, partner_factors = lax.optimization_barrier((leaf_full, leaf_tri, partner_factors))
    leaf_vectors = unit_lower(leaf_full)
    leaf_factor = jnp.triu(leaf_tri)
    leaf_w = product_left_t(leaf_factor, product_left_t(leaf_vectors, slab))
    leafed = slab - product(leaf_vectors, leaf_w)
    current = leafed[:width]

    is_lower = core == 0
    received = lax.ppermute(current, "row", swap)
    own_h = lax.dynamic_slice(current, (0, core * half), (width, half))
    early = product_left_t(jnp.where(is_lower, odd3[1], odd3[2]), own_h)
    early, received = lax.optimization_barrier((early, received))
    recv_h = lax.dynamic_slice(received, (0, core * half), (width, half))
    update = early + product_left_t(jnp.where(is_lower, odd3[2], odd3[1]), recv_h)
    upper_h = jnp.where(is_lower, recv_h, own_h)
    level0_out = upper_h - product(odd3[0], update)
    chain = jnp.where(is_lower, own_h, recv_h) - update

    zeros = jnp.zeros_like(tree_factor)
    result = chain
    for level in range(1, levels):
        step = 1 << level
        phase = base % (2 * step)
        is_lower = phase == 0
        is_upper = phase == step
        pairs = []
        for i in range(0, n_row, 2 * step):
            for c in range(2):
                pairs += [(i + c, i + step + c), (i + step + c, i + c)]
        q = product_left_t(jnp.where(is_upper, even3[2], zeros), chain)
        received = lax.ppermute(jnp.where(is_upper, q, chain), "row", pairs)
        mine = partner_factors[level - 1]
        mates = lax.ppermute(mine, "row", swap)
        top_rows = jnp.where(is_lower & (core == 0), mine, jnp.where(is_lower, mates, 0.0))
        bottom_rows = jnp.where(is_lower & (core == 0), mates, jnp.where(is_lower, mine, 0.0))
        own_part = product_left_t(top_rows, chain[:hw]) + product_left_t(bottom_rows, chain[hw:])
        own_part, received = lax.optimization_barrier((own_part, received))
        update = product_left_t(even3[1], received) + q
        result = jnp.where(is_upper, chain - product(even3[0], update), result)
        chain = jnp.where(is_lower, chain - own_part - received, chain)
    base_out = jnp.where(base == 0, chain, result)

    keep = jnp.where(core == 0, base_out, level0_out)
    give = jnp.where(core == 0, level0_out, base_out)
    got = lax.ppermute(give, "row", swap)
    top = jnp.concatenate([jnp.where(core == 0, keep, got), jnp.where(core == 0, got, keep)], axis=1)
    return jnp.concatenate([top, leafed[width:]], axis=0)


def solution(mesh):
    in_specs = (P("row", "col"), P("row", "col"), P("row", "col"), P("row", "col"), P("row", "col"))
    out_specs = P("row", "col")
    return jax.shard_map(
        on_device, mesh=mesh, in_specs=in_specs, out_specs=out_specs, check_vma=False
    )
```

```python
import jax
import jax.numpy as jnp
from jax import lax
from jax.sharding import PartitionSpec as P


def product(left, right):
    return jnp.dot(left, right, precision=lax.Precision.HIGH, preferred_element_type=jnp.float32)


def product_left_t(left, right):
    return lax.dot_general(
        left,
        right,
        (((0,), (0,)), ((), ())),
        precision=lax.Precision.HIGH,
        preferred_element_type=jnp.float32,
    )


def unit_lower(raw):
    row_ids = lax.broadcasted_iota(jnp.int32, raw.shape, 0)
    col_ids = lax.broadcasted_iota(jnp.int32, raw.shape, 1)
    diagonal = jnp.where(row_ids == col_ids, 1.0, 0.0).astype(raw.dtype)
    return jnp.where(row_ids > col_ids, raw, 0.0) + diagonal


def col_gather(part):
    n_col = lax.axis_size("col")
    me = lax.axis_index("col")
    by_shift = [part]
    for shift in range(1, n_col):
        perm = [(i, (i + shift) % n_col) for i in range(n_col)]
        by_shift.append(lax.ppermute(part, "col", perm))
    stacked = jnp.stack(by_shift)
    blocks = [stacked[(me - b) % n_col] for b in range(n_col)]
    return jnp.concatenate(blocks, axis=1)


def on_device(slab, leaf_v, leaf_t, tree_v, tree_t):
    n_row = lax.axis_size("row")
    levels = n_row.bit_length() - 1
    position = lax.axis_index("row")
    rows = leaf_v.shape[0]
    width = leaf_t.shape[0]

    tree_tri = col_gather(tree_t)
    tree_tri, leaf_v, leaf_t, tree_v = lax.optimization_barrier((tree_tri, leaf_v, leaf_t, tree_v))
    leaf_full = col_gather(leaf_v)
    leaf_tri = col_gather(leaf_t)
    tree_full = col_gather(tree_v)

    tree_vectors = jnp.triu(tree_full)
    tree_factor = jnp.triu(tree_tri)
    tree_joint = product(tree_vectors, tree_factor)
    own3 = jnp.stack([tree_vectors, tree_factor, tree_joint])

    core = position % 2
    base = position - core
    cols = slab.shape[1]
    half = cols // 2
    swap = [(p, p ^ 1) for p in range(n_row)]
    mate3 = lax.ppermute(own3, "row", swap)
    even3 = jnp.where(core == 0, own3, mate3)

    hw = width // 2
    mate_s = lax.ppermute(tree_factor[hw:], "row", swap)
    half_s = jnp.where(core == 0, tree_factor[:hw], mate_s)
    partner_factors = []
    for level in range(1, levels):
        step = 1 << level
        pairs = []
        for i in range(0, n_row, 2 * step):
            pairs += [(i + step, i), (i + step + 1, i + 1)]
        partner_factors.append(lax.ppermute(half_s, "row", pairs))

    leaf_full, leaf_tri, partner_factors = lax.optimization_barrier((leaf_full, leaf_tri, partner_factors))
    leaf_vectors = unit_lower(leaf_full)
    leaf_factor = jnp.triu(leaf_tri)
    leaf_w = product_left_t(leaf_factor, product_left_t(leaf_vectors, slab))
    leafed = slab - product(leaf_vectors, leaf_w)
    current = leafed[:width]

    is_lower = core == 0
    received = lax.ppermute(current, "row", swap)
    own_h = lax.dynamic_slice(current, (0, core * half), (width, half))
    early = product_left_t(jnp.where(is_lower, mate3[1], own3[2]), own_h)
    early, received = lax.optimization_barrier((early, received))
    recv_h = lax.dynamic_slice(received, (0, core * half), (width, half))
    update = early + product_left_t(jnp.where(is_lower, mate3[2], own3[1]), recv_h)
    upper_h = jnp.where(is_lower, recv_h, own_h)
    level0_out = upper_h - product(jnp.where(is_lower, mate3[0], own3[0]), update)
    chain = jnp.where(is_lower, own_h, recv_h) - update

    zeros = jnp.zeros_like(tree_factor)
    result = chain
    for level in range(1, levels):
        step = 1 << level
        phase = base % (2 * step)
        is_lower = phase == 0
        is_upper = phase == step
        pairs = []
        for i in range(0, n_row, 2 * step):
            for c in range(2):
                pairs += [(i + c, i + step + c), (i + step + c, i + c)]
        q = product_left_t(jnp.where(is_upper, even3[2], zeros), chain)
        received = lax.ppermute(jnp.where(is_upper, q, chain), "row", pairs)
        mine = partner_factors[level - 1]
        mates = lax.ppermute(mine, "row", swap)
        top_rows = jnp.where(is_lower & (core == 0), mine, jnp.where(is_lower, mates, 0.0))
        bottom_rows = jnp.where(is_lower & (core == 0), mates, jnp.where(is_lower, mine, 0.0))
        own_part = product_left_t(top_rows, chain[:hw]) + product_left_t(bottom_rows, chain[hw:])
        own_part, received = lax.optimization_barrier((own_part, received))
        update = product_left_t(even3[1], received) + q
        result = jnp.where(is_upper, chain - product(even3[0], update), result)
        chain = jnp.where(is_lower, chain - own_part - received, chain)
    base_out = jnp.where(base == 0, chain, result)

    keep = jnp.where(core == 0, base_out, level0_out)
    give = jnp.where(core == 0, level0_out, base_out)
    got = lax.ppermute(give, "row", swap)
    top = jnp.concatenate([jnp.where(core == 0, keep, got), jnp.where(core == 0, got, keep)], axis=1)
    return jnp.concatenate([top, leafed[width:]], axis=0)


def solution(mesh):
    in_specs = (P("row", "col"), P("row", "col"), P("row", "col"), P("row", "col"), P("row", "col"))
    out_specs = P("row", "col")
    return jax.shard_map(
        on_device, mesh=mesh, in_specs=in_specs, out_specs=out_specs, check_vma=False
    )
```

```python
import jax
import jax.numpy as jnp
from jax import lax
from jax.sharding import PartitionSpec as P


def product(left, right):
    return jnp.dot(left, right, precision=lax.Precision.HIGH, preferred_element_type=jnp.float32)


def product_left_t(left, right):
    return lax.dot_general(
        left,
        right,
        (((0,), (0,)), ((), ())),
        precision=lax.Precision.HIGH,
        preferred_element_type=jnp.float32,
    )


def unit_lower(raw):
    row_ids = lax.broadcasted_iota(jnp.int32, raw.shape, 0)
    col_ids = lax.broadcasted_iota(jnp.int32, raw.shape, 1)
    diagonal = jnp.where(row_ids == col_ids, 1.0, 0.0).astype(raw.dtype)
    return jnp.where(row_ids > col_ids, raw, 0.0) + diagonal


def col_gather(part):
    n_col = lax.axis_size("col")
    me = lax.axis_index("col")
    by_shift = [part]
    for shift in range(1, n_col):
        perm = [(i, (i + shift) % n_col) for i in range(n_col)]
        by_shift.append(lax.ppermute(part, "col", perm))
    stacked = jnp.stack(by_shift)
    blocks = [stacked[(me - b) % n_col] for b in range(n_col)]
    return jnp.concatenate(blocks, axis=1)


def on_device(slab, leaf_v, leaf_t, tree_v, tree_t):
    n_row = lax.axis_size("row")
    levels = n_row.bit_length() - 1
    position = lax.axis_index("row")
    rows = leaf_v.shape[0]
    width = leaf_t.shape[0]

    tree_tri = col_gather(tree_t)
    tree_tri, leaf_v, leaf_t, tree_v = lax.optimization_barrier((tree_tri, leaf_v, leaf_t, tree_v))
    leaf_full = col_gather(leaf_v)
    leaf_tri = col_gather(leaf_t)
    tree_full = col_gather(tree_v)

    tree_vectors = jnp.triu(tree_full)
    tree_factor = jnp.triu(tree_tri)
    tree_joint = product(tree_vectors, tree_factor)
    own3 = jnp.stack([tree_vectors, tree_factor, tree_joint])

    core = position % 2
    base = position - core
    cols = slab.shape[1]
    half = cols // 2
    swap = [(p, p ^ 1) for p in range(n_row)]
    mate3 = lax.ppermute(own3, "row", swap)
    odd3 = jnp.where(core == 1, own3, mate3)
    even3 = jnp.where(core == 0, own3, mate3)

    hw = width // 2
    mate_s = lax.ppermute(tree_factor[hw:], "row", swap)
    half_s = jnp.where(core == 0, tree_factor[:hw], mate_s)
    partner_factors = []
    for level in range(1, levels):
        step = 1 << level
        pairs = []
        for i in range(0, n_row, 2 * step):
            pairs += [(i + step, i), (i + step + 1, i + 1)]
        partner_factors.append(lax.ppermute(half_s, "row", pairs))

    mates_of = [lax.ppermute(got, "row", swap) for got in partner_factors]
    leaf_full, leaf_tri, partner_factors, mates_of = lax.optimization_barrier(
        (leaf_full, leaf_tri, partner_factors, mates_of)
    )
    leaf_vectors = unit_lower(leaf_full)
    leaf_factor = jnp.triu(leaf_tri)
    leaf_w = product_left_t(leaf_factor, product_left_t(leaf_vectors, slab))
    current = slab[:width] - product(leaf_vectors[:width], leaf_w)
    remainder = slab[width:] - product(leaf_vectors[width:], leaf_w)

    is_lower = core == 0
    received = lax.ppermute(current, "row", swap)
    own_h = lax.dynamic_slice(current, (0, core * half), (width, half))
    early = product_left_t(jnp.where(is_lower, odd3[1], odd3[2]), own_h)
    early, received = lax.optimization_barrier((early, received))
    recv_h = lax.dynamic_slice(received, (0, core * half), (width, half))
    update = early + product_left_t(jnp.where(is_lower, odd3[2], odd3[1]), recv_h)
    upper_h = jnp.where(is_lower, recv_h, own_h)
    level0_out = upper_h - product(odd3[0], update)
    chain = jnp.where(is_lower, own_h, recv_h) - update

    zeros = jnp.zeros_like(tree_factor)
    result = chain
    for level in range(1, levels):
        step = 1 << level
        phase = base % (2 * step)
        is_lower = phase == 0
        is_upper = phase == step
        pairs = []
        for i in range(0, n_row, 2 * step):
            for c in range(2):
                pairs += [(i + c, i + step + c), (i + step + c, i + c)]
        q = product_left_t(jnp.where(is_upper, even3[2], zeros), chain)
        received = lax.ppermute(jnp.where(is_upper, q, chain), "row", pairs)
        mine = partner_factors[level - 1]
        mates = mates_of[level - 1]
        top_rows = jnp.where(is_lower & (core == 0), mine, jnp.where(is_lower, mates, 0.0))
        bottom_rows = jnp.where(is_lower & (core == 0), mates, jnp.where(is_lower, mine, 0.0))
        own_part = product_left_t(top_rows, chain[:hw]) + product_left_t(bottom_rows, chain[hw:])
        own_part, received = lax.optimization_barrier((own_part, received))
        update = product_left_t(even3[1], received) + q
        result = jnp.where(is_upper, chain - product(even3[0], update), result)
        chain = jnp.where(is_lower, chain - own_part - received, chain)
    base_out = jnp.where(base == 0, chain, result)

    keep = jnp.where(core == 0, base_out, level0_out)
    give = jnp.where(core == 0, level0_out, base_out)
    got = lax.ppermute(give, "row", swap)
    top = jnp.concatenate([jnp.where(core == 0, keep, got), jnp.where(core == 0, got, keep)], axis=1)
    return jnp.concatenate([top, remainder], axis=0)


def solution(mesh):
    in_specs = (P("row", "col"), P("row", "col"), P("row", "col"), P("row", "col"), P("row", "col"))
    out_specs = P("row", "col")
    return jax.shard_map(
        on_device, mesh=mesh, in_specs=in_specs, out_specs=out_specs, check_vma=False
    )
```

```python
import jax
import jax.numpy as jnp
from jax import lax
from jax.sharding import PartitionSpec as P


def product(left, right):
    return jnp.dot(left, right, precision=lax.Precision.HIGH, preferred_element_type=jnp.float32)


def product_left_t(left, right):
    return lax.dot_general(
        left,
        right,
        (((0,), (0,)), ((), ())),
        precision=lax.Precision.HIGH,
        preferred_element_type=jnp.float32,
    )


def unit_lower(raw):
    row_ids = lax.broadcasted_iota(jnp.int32, raw.shape, 0)
    col_ids = lax.broadcasted_iota(jnp.int32, raw.shape, 1)
    diagonal = jnp.where(row_ids == col_ids, 1.0, 0.0).astype(raw.dtype)
    return jnp.where(row_ids > col_ids, raw, 0.0) + diagonal


def col_gather(part):
    n_col = lax.axis_size("col")
    me = lax.axis_index("col")
    by_shift = [part]
    for shift in range(1, n_col):
        perm = [(i, (i + shift) % n_col) for i in range(n_col)]
        by_shift.append(lax.ppermute(part, "col", perm))
    stacked = jnp.stack(by_shift)
    blocks = [stacked[(me - b) % n_col] for b in range(n_col)]
    return jnp.concatenate(blocks, axis=1)


def on_device(slab, leaf_v, leaf_t, tree_v, tree_t):
    n_row = lax.axis_size("row")
    levels = n_row.bit_length() - 1
    position = lax.axis_index("row")
    rows = leaf_v.shape[0]
    width = leaf_t.shape[0]

    tree_tri = col_gather(tree_t)
    tree_tri, leaf_v, leaf_t, tree_v = lax.optimization_barrier((tree_tri, leaf_v, leaf_t, tree_v))
    leaf_full = col_gather(leaf_v)
    leaf_tri = col_gather(leaf_t)
    tree_full = col_gather(tree_v)

    tree_vectors = jnp.triu(tree_full)
    tree_factor = jnp.triu(tree_tri)
    tree_joint = product(tree_vectors, tree_factor)
    own3 = jnp.stack([tree_vectors, tree_factor, tree_joint])

    core = position % 2
    base = position - core
    cols = slab.shape[1]
    half = cols // 2
    swap = [(p, p ^ 1) for p in range(n_row)]
    mate3 = lax.ppermute(own3, "row", swap)
    odd3 = jnp.where(core == 1, own3, mate3)
    even3 = jnp.where(core == 0, own3, mate3)

    hw = width // 2
    mate_s = lax.ppermute(tree_factor[hw:], "row", swap)
    half_s = jnp.where(core == 0, tree_factor[:hw], mate_s)
    partner_factors = []
    for level in range(1, levels):
        step = 1 << level
        pairs = []
        for i in range(0, n_row, 2 * step):
            pairs += [(i + step, i), (i + step + 1, i + 1)]
        partner_factors.append(lax.ppermute(half_s, "row", pairs))

    leaf_full, leaf_tri, partner_factors = lax.optimization_barrier((leaf_full, leaf_tri, partner_factors))
    leaf_vectors = unit_lower(leaf_full)
    leaf_factor = jnp.triu(leaf_tri)
    leaf_w = product_left_t(leaf_factor, product_left_t(leaf_vectors, slab))
    leafed = slab - product(leaf_vectors, leaf_w)
    current = leafed[:width]

    is_lower = core == 0
    received = lax.ppermute(current, "row", swap)
    own_h = lax.dynamic_slice(current, (0, core * half), (width, half))
    early = product_left_t(jnp.where(is_lower, odd3[1], odd3[2]), own_h)
    early, received = lax.optimization_barrier((early, received))
    recv_h = lax.dynamic_slice(received, (0, core * half), (width, half))
    update = early + product_left_t(jnp.where(is_lower, odd3[2], odd3[1]), recv_h)
    upper_h = jnp.where(is_lower, recv_h, own_h)
    level0_out = upper_h - product(odd3[0], update)
    chain = jnp.where(is_lower, own_h, recv_h) - update

    zeros = jnp.zeros_like(tree_factor)
    result = chain
    for level in range(1, levels):
        step = 1 << level
        phase = base % (2 * step)
        is_lower = phase == 0
        is_upper = phase == step
        pairs = []
        for i in range(0, n_row, 2 * step):
            for c in range(2):
                pairs += [(i + c, i + step + c), (i + step + c, i + c)]
        q = product_left_t(jnp.where(is_upper, even3[2], zeros), chain)
        received = lax.ppermute(jnp.where(is_upper, q, chain), "row", pairs)
        mine = partner_factors[level - 1]
        mates = lax.ppermute(mine, "row", swap)
        top_rows = jnp.where(is_lower & (core == 0), mine, jnp.where(is_lower, mates, 0.0))
        bottom_rows = jnp.where(is_lower & (core == 0), mates, jnp.where(is_lower, mine, 0.0))
        own_part = product_left_t(top_rows, chain[:hw]) + product_left_t(bottom_rows, chain[hw:])
        own_part, received = lax.optimization_barrier((own_part, received))
        if level == levels - 1:
            result = lax.cond(
                is_upper,
                lambda c, r, qq, old: c - product(even3[0], product_left_t(even3[1], r) + qq),
                lambda c, r, qq, old: old,
                chain,
                received,
                q,
                result,
            )
        else:
            update = product_left_t(even3[1], received) + q
            result = jnp.where(is_upper, chain - product(even3[0], update), result)
        chain = jnp.where(is_lower, chain - own_part - received, chain)
    base_out = jnp.where(base == 0, chain, result)

    keep = jnp.where(core == 0, base_out, level0_out)
    give = jnp.where(core == 0, level0_out, base_out)
    got = lax.ppermute(give, "row", swap)
    top = jnp.concatenate([jnp.where(core == 0, keep, got), jnp.where(core == 0, got, keep)], axis=1)
    return jnp.concatenate([top, leafed[width:]], axis=0)


def solution(mesh):
    in_specs = (P("row", "col"), P("row", "col"), P("row", "col"), P("row", "col"), P("row", "col"))
    out_specs = P("row", "col")
    return jax.shard_map(
        on_device, mesh=mesh, in_specs=in_specs, out_specs=out_specs, check_vma=False
    )
```

```python
import jax
import jax.numpy as jnp
from jax import lax
from jax.sharding import PartitionSpec as P


def product(left, right):
    return jnp.dot(left, right, precision=lax.Precision.HIGH, preferred_element_type=jnp.float32)


def product_left_t(left, right):
    return lax.dot_general(
        left,
        right,
        (((0,), (0,)), ((), ())),
        precision=lax.Precision.HIGH,
        preferred_element_type=jnp.float32,
    )


def unit_lower(raw):
    row_ids = lax.broadcasted_iota(jnp.int32, raw.shape, 0)
    col_ids = lax.broadcasted_iota(jnp.int32, raw.shape, 1)
    diagonal = jnp.where(row_ids == col_ids, 1.0, 0.0).astype(raw.dtype)
    return jnp.where(row_ids > col_ids, raw, 0.0) + diagonal


def col_gather(part):
    n_col = lax.axis_size("col")
    me = lax.axis_index("col")
    by_shift = [part]
    for shift in range(1, n_col):
        perm = [(i, (i + shift) % n_col) for i in range(n_col)]
        by_shift.append(lax.ppermute(part, "col", perm))
    stacked = jnp.stack(by_shift)
    blocks = [stacked[(me - b) % n_col] for b in range(n_col)]
    return jnp.concatenate(blocks, axis=1)


def on_device(slab, leaf_v, leaf_t, tree_v, tree_t):
    n_row = lax.axis_size("row")
    levels = n_row.bit_length() - 1
    position = lax.axis_index("row")
    rows = leaf_v.shape[0]
    width = leaf_t.shape[0]

    tree_tri = col_gather(tree_t)
    tree_tri, leaf_v, leaf_t, tree_v = lax.optimization_barrier((tree_tri, leaf_v, leaf_t, tree_v))
    leaf_full = col_gather(leaf_v)
    leaf_tri = col_gather(leaf_t)
    tree_full = col_gather(tree_v)

    tree_vectors = jnp.triu(tree_full)
    tree_factor = jnp.triu(tree_tri)
    tree_joint = product(tree_vectors, tree_factor)
    own3 = jnp.stack([tree_vectors, tree_factor, tree_joint])

    core = position % 2
    base = position - core
    cols = slab.shape[1]
    half = cols // 2
    swap = [(p, p ^ 1) for p in range(n_row)]
    mate3 = lax.ppermute(own3, "row", swap)
    odd3 = jnp.where(core == 1, own3, mate3)
    even3 = jnp.where(core == 0, own3, mate3)

    hw = width // 2
    mate_s = lax.ppermute(tree_factor[hw:], "row", swap)
    half_s = jnp.where(core == 0, tree_factor[:hw], mate_s)
    partner_factors = []
    for level in range(1, levels):
        step = 1 << level
        pairs = []
        for i in range(0, n_row, 2 * step):
            pairs += [(i + step, i), (i + step + 1, i + 1)]
        partner_factors.append(lax.ppermute(half_s, "row", pairs))

    leaf_full, leaf_tri, partner_factors = lax.optimization_barrier((leaf_full, leaf_tri, partner_factors))
    leaf_vectors = unit_lower(leaf_full)
    leaf_factor = jnp.triu(leaf_tri)
    leaf_w = product_left_t(leaf_factor, product_left_t(leaf_vectors, slab))
    leafed = slab - product(leaf_vectors, leaf_w)
    current = leafed[:width]

    is_lower = core == 0
    recv_h = lax.ppermute(lax.dynamic_slice(current, (0, (1 - core) * half), (width, half)), "row", swap)
    own_h = lax.dynamic_slice(current, (0, core * half), (width, half))
    early = product_left_t(jnp.where(is_lower, odd3[1], odd3[2]), own_h)
    early, recv_h = lax.optimization_barrier((early, recv_h))
    update = early + product_left_t(jnp.where(is_lower, odd3[2], odd3[1]), recv_h)
    upper_h = jnp.where(is_lower, recv_h, own_h)
    level0_out = upper_h - product(odd3[0], update)
    chain = jnp.where(is_lower, own_h, recv_h) - update

    zeros = jnp.zeros_like(tree_factor)
    result = chain
    for level in range(1, levels):
        step = 1 << level
        phase = base % (2 * step)
        is_lower = phase == 0
        is_upper = phase == step
        pairs = []
        for i in range(0, n_row, 2 * step):
            for c in range(2):
                pairs += [(i + c, i + step + c), (i + step + c, i + c)]
        q = product_left_t(jnp.where(is_upper, even3[2], zeros), chain)
        received = lax.ppermute(jnp.where(is_upper, q, chain), "row", pairs)
        mine = partner_factors[level - 1]
        mates = lax.ppermute(mine, "row", swap)
        top_rows = jnp.where(is_lower & (core == 0), mine, jnp.where(is_lower, mates, 0.0))
        bottom_rows = jnp.where(is_lower & (core == 0), mates, jnp.where(is_lower, mine, 0.0))
        own_part = product_left_t(top_rows, chain[:hw]) + product_left_t(bottom_rows, chain[hw:])
        own_part, received = lax.optimization_barrier((own_part, received))
        update = product_left_t(even3[1], received) + q
        result = jnp.where(is_upper, chain - product(even3[0], update), result)
        chain = jnp.where(is_lower, chain - own_part - received, chain)
    base_out = jnp.where(base == 0, chain, result)

    keep = jnp.where(core == 0, base_out, level0_out)
    give = jnp.where(core == 0, level0_out, base_out)
    got = lax.ppermute(give, "row", swap)
    top = jnp.concatenate([jnp.where(core == 0, keep, got), jnp.where(core == 0, got, keep)], axis=1)
    return jnp.concatenate([top, leafed[width:]], axis=0)


def solution(mesh):
    in_specs = (P("row", "col"), P("row", "col"), P("row", "col"), P("row", "col"), P("row", "col"))
    out_specs = P("row", "col")
    return jax.shard_map(
        on_device, mesh=mesh, in_specs=in_specs, out_specs=out_specs, check_vma=False
    )
```

```python
import jax
import jax.numpy as jnp
from jax import lax
from jax.sharding import PartitionSpec as P


def product(left, right):
    return jnp.dot(left, right, precision=lax.Precision.HIGH, preferred_element_type=jnp.float32)


def product_left_t(left, right):
    return lax.dot_general(
        left,
        right,
        (((0,), (0,)), ((), ())),
        precision=lax.Precision.HIGH,
        preferred_element_type=jnp.float32,
    )


def unit_lower(raw):
    row_ids = lax.broadcasted_iota(jnp.int32, raw.shape, 0)
    col_ids = lax.broadcasted_iota(jnp.int32, raw.shape, 1)
    diagonal = jnp.where(row_ids == col_ids, 1.0, 0.0).astype(raw.dtype)
    return jnp.where(row_ids > col_ids, raw, 0.0) + diagonal


def col_gather(part):
    n_col = lax.axis_size("col")
    me = lax.axis_index("col")
    by_shift = [part]
    for shift in range(1, n_col):
        perm = [(i, (i + shift) % n_col) for i in range(n_col)]
        by_shift.append(lax.ppermute(part, "col", perm))
    if n_col == 2:
        first = jnp.where(me == 0, part, by_shift[1])
        second = jnp.where(me == 0, by_shift[1], part)
        return jnp.concatenate([first, second], axis=1)
    stacked = jnp.stack(by_shift)
    blocks = [stacked[(me - b) % n_col] for b in range(n_col)]
    return jnp.concatenate(blocks, axis=1)


def on_device(slab, leaf_v, leaf_t, tree_v, tree_t):
    n_row = lax.axis_size("row")
    levels = n_row.bit_length() - 1
    position = lax.axis_index("row")
    rows = leaf_v.shape[0]
    width = leaf_t.shape[0]

    tree_tri = col_gather(tree_t)
    tree_tri, leaf_v, leaf_t, tree_v = lax.optimization_barrier((tree_tri, leaf_v, leaf_t, tree_v))
    leaf_full = col_gather(leaf_v)
    leaf_tri = col_gather(leaf_t)
    tree_full = col_gather(tree_v)

    tree_vectors = jnp.triu(tree_full)
    tree_factor = jnp.triu(tree_tri)
    tree_joint = product(tree_vectors, tree_factor)
    own3 = jnp.stack([tree_vectors, tree_factor, tree_joint])

    core = position % 2
    base = position - core
    cols = slab.shape[1]
    half = cols // 2
    swap = [(p, p ^ 1) for p in range(n_row)]
    mate3 = lax.ppermute(own3, "row", swap)
    odd3 = jnp.where(core == 1, own3, mate3)
    even3 = jnp.where(core == 0, own3, mate3)

    hw = width // 2
    mate_s = lax.ppermute(tree_factor[hw:], "row", swap)
    half_s = jnp.where(core == 0, tree_factor[:hw], mate_s)
    partner_factors = []
    for level in range(1, levels):
        step = 1 << level
        pairs = []
        for i in range(0, n_row, 2 * step):
            pairs += [(i + step, i), (i + step + 1, i + 1)]
        partner_factors.append(lax.ppermute(half_s, "row", pairs))

    leaf_full, leaf_tri, partner_factors = lax.optimization_barrier((leaf_full, leaf_tri, partner_factors))
    leaf_vectors = unit_lower(leaf_full)
    leaf_factor = jnp.triu(leaf_tri)
    leaf_w = product_left_t(leaf_factor, product_left_t(leaf_vectors, slab))
    leafed = slab - product(leaf_vectors, leaf_w)
    current = leafed[:width]

    is_lower = core == 0
    recv_h = lax.ppermute(lax.dynamic_slice(current, (0, (1 - core) * half), (width, half)), "row", swap)
    own_h = lax.dynamic_slice(current, (0, core * half), (width, half))
    early = product_left_t(jnp.where(is_lower, odd3[1], odd3[2]), own_h)
    early, recv_h = lax.optimization_barrier((early, recv_h))
    update = early + product_left_t(jnp.where(is_lower, odd3[2], odd3[1]), recv_h)
    upper_h = jnp.where(is_lower, recv_h, own_h)
    level0_out = upper_h - product(odd3[0], update)
    chain = jnp.where(is_lower, own_h, recv_h) - update

    zeros = jnp.zeros_like(tree_factor)
    result = chain
    for level in range(1, levels):
        step = 1 << level
        phase = base % (2 * step)
        is_lower = phase == 0
        is_upper = phase == step
        pairs = []
        for i in range(0, n_row, 2 * step):
            for c in range(2):
                pairs += [(i + c, i + step + c), (i + step + c, i + c)]
        q = product_left_t(jnp.where(is_upper, even3[2], zeros), chain)
        received = lax.ppermute(jnp.where(is_upper, q, chain), "row", pairs)
        mine = partner_factors[level - 1]
        mates = lax.ppermute(mine, "row", swap)
        top_rows = jnp.where(is_lower & (core == 0), mine, jnp.where(is_lower, mates, 0.0))
        bottom_rows = jnp.where(is_lower & (core == 0), mates, jnp.where(is_lower, mine, 0.0))
        own_part = product_left_t(top_rows, chain[:hw]) + product_left_t(bottom_rows, chain[hw:])
        own_part, received = lax.optimization_barrier((own_part, received))
        update = product_left_t(even3[1], received) + q
        result = jnp.where(is_upper, chain - product(even3[0], update), result)
        chain = jnp.where(is_lower, chain - own_part - received, chain)
    base_out = jnp.where(base == 0, chain, result)

    keep = jnp.where(core == 0, base_out, level0_out)
    give = jnp.where(core == 0, level0_out, base_out)
    got = lax.ppermute(give, "row", swap)
    top = jnp.concatenate([jnp.where(core == 0, keep, got), jnp.where(core == 0, got, keep)], axis=1)
    return jnp.concatenate([top, leafed[width:]], axis=0)


def solution(mesh):
    in_specs = (P("row", "col"), P("row", "col"), P("row", "col"), P("row", "col"), P("row", "col"))
    out_specs = P("row", "col")
    return jax.shard_map(
        on_device, mesh=mesh, in_specs=in_specs, out_specs=out_specs, check_vma=False
    )
```

```python
import jax
import jax.numpy as jnp
from jax import lax
from jax.sharding import PartitionSpec as P


def product(left, right):
    return jnp.dot(left, right, precision=lax.Precision.HIGH, preferred_element_type=jnp.float32)


def product_left_t(left, right):
    return lax.dot_general(
        left,
        right,
        (((0,), (0,)), ((), ())),
        precision=lax.Precision.HIGH,
        preferred_element_type=jnp.float32,
    )


def unit_lower(raw):
    row_ids = lax.broadcasted_iota(jnp.int32, raw.shape, 0)
    col_ids = lax.broadcasted_iota(jnp.int32, raw.shape, 1)
    diagonal = jnp.where(row_ids == col_ids, 1.0, 0.0).astype(raw.dtype)
    return jnp.where(row_ids > col_ids, raw, 0.0) + diagonal


def col_gather(part):
    n_col = lax.axis_size("col")
    me = lax.axis_index("col")
    by_shift = [part]
    for shift in range(1, n_col):
        perm = [(i, (i + shift) % n_col) for i in range(n_col)]
        by_shift.append(lax.ppermute(part, "col", perm))
    if n_col == 2:
        first = jnp.where(me == 0, part, by_shift[1])
        second = jnp.where(me == 0, by_shift[1], part)
        return jnp.concatenate([first, second], axis=1)
    stacked = jnp.stack(by_shift)
    blocks = [stacked[(me - b) % n_col] for b in range(n_col)]
    return jnp.concatenate(blocks, axis=1)


def on_device(slab, leaf_v, leaf_t, tree_v, tree_t):
    n_row = lax.axis_size("row")
    levels = n_row.bit_length() - 1
    position = lax.axis_index("row")
    rows = leaf_v.shape[0]
    width = leaf_t.shape[0]

    tree_tri = col_gather(tree_t)
    tree_tri, leaf_v, leaf_t, tree_v = lax.optimization_barrier((tree_tri, leaf_v, leaf_t, tree_v))
    leaf_full = col_gather(leaf_v)
    leaf_tri = col_gather(leaf_t)
    tree_full = col_gather(tree_v)

    tree_vectors = jnp.triu(tree_full)
    tree_factor = jnp.triu(tree_tri)
    tree_joint = product(tree_vectors, tree_factor)
    own3 = jnp.stack([tree_vectors, tree_factor, tree_joint])

    core = position % 2
    base = position - core
    cols = slab.shape[1]
    half = cols // 2
    swap = [(p, p ^ 1) for p in range(n_row)]
    mate3 = lax.ppermute(own3, "row", swap)
    odd3 = jnp.where(core == 1, own3, mate3)
    even3 = jnp.where(core == 0, own3, mate3)

    hw = width // 2
    mate_s = lax.ppermute(tree_factor[hw:], "row", swap)
    half_s = jnp.where(core == 0, tree_factor[:hw], mate_s)
    partner_factors = []
    for level in range(1, levels):
        step = 1 << level
        pairs = []
        for i in range(0, n_row, 2 * step):
            pairs += [(i + step, i), (i + step + 1, i + 1)]
        partner_factors.append(lax.ppermute(half_s, "row", pairs))

    mates_of = [lax.ppermute(got, "row", swap) for got in partner_factors]
    leaf_full, leaf_tri, partner_factors, mates_of = lax.optimization_barrier(
        (leaf_full, leaf_tri, partner_factors, mates_of)
    )
    leaf_vectors = unit_lower(leaf_full)
    leaf_factor = jnp.triu(leaf_tri)
    leaf_w = product_left_t(leaf_factor, product_left_t(leaf_vectors, slab))
    leafed = slab - product(leaf_vectors, leaf_w)
    current = leafed[:width]

    is_lower = core == 0
    recv_h = lax.ppermute(lax.dynamic_slice(current, (0, (1 - core) * half), (width, half)), "row", swap)
    own_h = lax.dynamic_slice(current, (0, core * half), (width, half))
    early = product_left_t(jnp.where(is_lower, odd3[1], odd3[2]), own_h)
    early, recv_h = lax.optimization_barrier((early, recv_h))
    update = early + product_left_t(jnp.where(is_lower, odd3[2], odd3[1]), recv_h)
    upper_h = jnp.where(is_lower, recv_h, own_h)
    level0_out = upper_h - product(odd3[0], update)
    chain = jnp.where(is_lower, own_h, recv_h) - update

    zeros = jnp.zeros_like(tree_factor)
    result = chain
    for level in range(1, levels):
        step = 1 << level
        phase = base % (2 * step)
        is_lower = phase == 0
        is_upper = phase == step
        pairs = []
        for i in range(0, n_row, 2 * step):
            for c in range(2):
                pairs += [(i + c, i + step + c), (i + step + c, i + c)]
        q = product_left_t(jnp.where(is_upper, even3[2], zeros), chain)
        received = lax.ppermute(jnp.where(is_upper, q, chain), "row", pairs)
        mine = partner_factors[level - 1]
        mates = mates_of[level - 1]
        top_rows = jnp.where(is_lower & (core == 0), mine, jnp.where(is_lower, mates, 0.0))
        bottom_rows = jnp.where(is_lower & (core == 0), mates, jnp.where(is_lower, mine, 0.0))
        own_part = product_left_t(top_rows, chain[:hw]) + product_left_t(bottom_rows, chain[hw:])
        own_part, received = lax.optimization_barrier((own_part, received))
        update = product_left_t(even3[1], received) + q
        result = jnp.where(is_upper, chain - product(even3[0], update), result)
        chain = jnp.where(is_lower, chain - own_part - received, chain)
    base_out = jnp.where(base == 0, chain, result)

    keep = jnp.where(core == 0, base_out, level0_out)
    give = jnp.where(core == 0, level0_out, base_out)
    got = lax.ppermute(give, "row", swap)
    top = jnp.concatenate([jnp.where(core == 0, keep, got), jnp.where(core == 0, got, keep)], axis=1)
    return jnp.concatenate([top, leafed[width:]], axis=0)


def solution(mesh):
    in_specs = (P("row", "col"), P("row", "col"), P("row", "col"), P("row", "col"), P("row", "col"))
    out_specs = P("row", "col")
    return jax.shard_map(
        on_device, mesh=mesh, in_specs=in_specs, out_specs=out_specs, check_vma=False
    )
```

```python
import jax
import jax.numpy as jnp
from jax import lax
from jax.sharding import PartitionSpec as P


def product(left, right):
    return jnp.dot(left, right, precision=lax.Precision.HIGH, preferred_element_type=jnp.float32)


def product_left_t(left, right):
    return lax.dot_general(
        left,
        right,
        (((0,), (0,)), ((), ())),
        precision=lax.Precision.HIGH,
        preferred_element_type=jnp.float32,
    )


def unit_lower(raw):
    row_ids = lax.broadcasted_iota(jnp.int32, raw.shape, 0)
    col_ids = lax.broadcasted_iota(jnp.int32, raw.shape, 1)
    diagonal = jnp.where(row_ids == col_ids, 1.0, 0.0).astype(raw.dtype)
    return jnp.where(row_ids > col_ids, raw, 0.0) + diagonal


def col_gather(part):
    n_col = lax.axis_size("col")
    me = lax.axis_index("col")
    by_shift = [part]
    for shift in range(1, n_col):
        perm = [(i, (i + shift) % n_col) for i in range(n_col)]
        by_shift.append(lax.ppermute(part, "col", perm))
    if n_col == 2:
        first = jnp.where(me == 0, part, by_shift[1])
        second = jnp.where(me == 0, by_shift[1], part)
        return jnp.concatenate([first, second], axis=1)
    stacked = jnp.stack(by_shift)
    blocks = [stacked[(me - b) % n_col] for b in range(n_col)]
    return jnp.concatenate(blocks, axis=1)


def on_device(slab, leaf_v, leaf_t, tree_v, tree_t):
    n_row = lax.axis_size("row")
    levels = n_row.bit_length() - 1
    position = lax.axis_index("row")
    rows = leaf_v.shape[0]
    width = leaf_t.shape[0]

    tree_tri = col_gather(tree_t)
    tree_tri, leaf_v, leaf_t, tree_v = lax.optimization_barrier((tree_tri, leaf_v, leaf_t, tree_v))
    leaf_full = col_gather(leaf_v)
    leaf_tri = col_gather(leaf_t)
    tree_full = col_gather(tree_v)

    tree_vectors = jnp.triu(tree_full)
    tree_factor = jnp.triu(tree_tri)
    tree_joint = product(tree_vectors, tree_factor)
    own3 = jnp.stack([tree_vectors, tree_factor, tree_joint])

    core = position % 2
    base = position - core
    cols = slab.shape[1]
    half = cols // 2
    swap = [(p, p ^ 1) for p in range(n_row)]
    mate3 = lax.ppermute(own3, "row", swap)
    odd3 = jnp.where(core == 1, own3, mate3)
    even3 = jnp.where(core == 0, own3, mate3)

    hw = width // 2
    mate_s = lax.ppermute(tree_factor[hw:], "row", swap)
    half_s = jnp.where(core == 0, tree_factor[:hw], mate_s)
    partner_factors = []
    for level in range(1, levels):
        step = 1 << level
        pairs = []
        for i in range(0, n_row, 2 * step):
            pairs += [(i + step, i), (i + step + 1, i + 1)]
        partner_factors.append(lax.ppermute(half_s, "row", pairs))

    leaf_full, leaf_tri, partner_factors = lax.optimization_barrier((leaf_full, leaf_tri, partner_factors))
    leaf_vectors = unit_lower(leaf_full)
    leaf_factor = jnp.triu(leaf_tri)
    leaf_w = product_left_t(leaf_factor, product_left_t(leaf_vectors, slab))
    current = slab[:width] - product(leaf_vectors[:width], leaf_w)
    remainder = slab[width:] - product(leaf_vectors[width:], leaf_w)

    is_lower = core == 0
    recv_h = lax.ppermute(lax.dynamic_slice(current, (0, (1 - core) * half), (width, half)), "row", swap)
    own_h = lax.dynamic_slice(current, (0, core * half), (width, half))
    early = product_left_t(jnp.where(is_lower, odd3[1], odd3[2]), own_h)
    early, recv_h = lax.optimization_barrier((early, recv_h))
    update = early + product_left_t(jnp.where(is_lower, odd3[2], odd3[1]), recv_h)
    upper_h = jnp.where(is_lower, recv_h, own_h)
    level0_out = upper_h - product(odd3[0], update)
    chain = jnp.where(is_lower, own_h, recv_h) - update

    zeros = jnp.zeros_like(tree_factor)
    result = chain
    for level in range(1, levels):
        step = 1 << level
        phase = base % (2 * step)
        is_lower = phase == 0
        is_upper = phase == step
        pairs = []
        for i in range(0, n_row, 2 * step):
            for c in range(2):
                pairs += [(i + c, i + step + c), (i + step + c, i + c)]
        q = product_left_t(jnp.where(is_upper, even3[2], zeros), chain)
        received = lax.ppermute(jnp.where(is_upper, q, chain), "row", pairs)
        mine = partner_factors[level - 1]
        mates = lax.ppermute(mine, "row", swap)
        top_rows = jnp.where(is_lower & (core == 0), mine, jnp.where(is_lower, mates, 0.0))
        bottom_rows = jnp.where(is_lower & (core == 0), mates, jnp.where(is_lower, mine, 0.0))
        own_part = product_left_t(top_rows, chain[:hw]) + product_left_t(bottom_rows, chain[hw:])
        own_part, received = lax.optimization_barrier((own_part, received))
        update = product_left_t(even3[1], received) + q
        result = jnp.where(is_upper, chain - product(even3[0], update), result)
        chain = jnp.where(is_lower, chain - own_part - received, chain)
    base_out = jnp.where(base == 0, chain, result)

    keep = jnp.where(core == 0, base_out, level0_out)
    give = jnp.where(core == 0, level0_out, base_out)
    got = lax.ppermute(give, "row", swap)
    top = jnp.concatenate([jnp.where(core == 0, keep, got), jnp.where(core == 0, got, keep)], axis=1)
    return jnp.concatenate([top, remainder], axis=0)


def solution(mesh):
    in_specs = (P("row", "col"), P("row", "col"), P("row", "col"), P("row", "col"), P("row", "col"))
    out_specs = P("row", "col")
    return jax.shard_map(
        on_device, mesh=mesh, in_specs=in_specs, out_specs=out_specs, check_vma=False
    )
```

```python
import jax
import jax.numpy as jnp
from jax import lax
from jax.sharding import PartitionSpec as P


def product(left, right):
    return jnp.dot(left, right, precision=lax.Precision.HIGH, preferred_element_type=jnp.float32)


def product_left_t(left, right):
    return lax.dot_general(
        left,
        right,
        (((0,), (0,)), ((), ())),
        precision=lax.Precision.HIGH,
        preferred_element_type=jnp.float32,
    )


def unit_lower(raw):
    row_ids = lax.broadcasted_iota(jnp.int32, raw.shape, 0)
    col_ids = lax.broadcasted_iota(jnp.int32, raw.shape, 1)
    diagonal = jnp.where(row_ids == col_ids, 1.0, 0.0).astype(raw.dtype)
    return jnp.where(row_ids > col_ids, raw, 0.0) + diagonal


def col_gather(part):
    n_col = lax.axis_size("col")
    me = lax.axis_index("col")
    by_shift = [part]
    for shift in range(1, n_col):
        perm = [(i, (i + shift) % n_col) for i in range(n_col)]
        by_shift.append(lax.ppermute(part, "col", perm))
    if n_col == 2:
        first = jnp.where(me == 0, part, by_shift[1])
        second = jnp.where(me == 0, by_shift[1], part)
        return jnp.concatenate([first, second], axis=1)
    stacked = jnp.stack(by_shift)
    blocks = [stacked[(me - b) % n_col] for b in range(n_col)]
    return jnp.concatenate(blocks, axis=1)


def on_device(slab, leaf_v, leaf_t, tree_v, tree_t):
    n_row = lax.axis_size("row")
    levels = n_row.bit_length() - 1
    position = lax.axis_index("row")
    rows = leaf_v.shape[0]
    width = leaf_t.shape[0]

    tree_tri = col_gather(tree_t)
    tree_full = col_gather(tree_v)
    tree_tri, tree_full, leaf_v, leaf_t = lax.optimization_barrier((tree_tri, tree_full, leaf_v, leaf_t))
    leaf_full = col_gather(leaf_v)
    leaf_tri = col_gather(leaf_t)

    tree_vectors = jnp.triu(tree_full)
    tree_factor = jnp.triu(tree_tri)
    tree_joint = product(tree_vectors, tree_factor)
    own3 = jnp.stack([tree_vectors, tree_factor, tree_joint])

    core = position % 2
    base = position - core
    cols = slab.shape[1]
    half = cols // 2
    swap = [(p, p ^ 1) for p in range(n_row)]
    mate3 = lax.ppermute(own3, "row", swap)
    odd3 = jnp.where(core == 1, own3, mate3)
    even3 = jnp.where(core == 0, own3, mate3)

    hw = width // 2
    mate_s = lax.ppermute(tree_factor[hw:], "row", swap)
    half_s = jnp.where(core == 0, tree_factor[:hw], mate_s)
    partner_factors = []
    for level in range(1, levels):
        step = 1 << level
        pairs = []
        for i in range(0, n_row, 2 * step):
            pairs += [(i + step, i), (i + step + 1, i + 1)]
        partner_factors.append(lax.ppermute(half_s, "row", pairs))

    leaf_full, leaf_tri, partner_factors = lax.optimization_barrier((leaf_full, leaf_tri, partner_factors))
    leaf_vectors = unit_lower(leaf_full)
    leaf_factor = jnp.triu(leaf_tri)
    leaf_w = product_left_t(leaf_factor, product_left_t(leaf_vectors, slab))
    current = slab[:width] - product(leaf_vectors[:width], leaf_w)
    remainder = slab[width:] - product(leaf_vectors[width:], leaf_w)

    is_lower = core == 0
    recv_h = lax.ppermute(lax.dynamic_slice(current, (0, (1 - core) * half), (width, half)), "row", swap)
    own_h = lax.dynamic_slice(current, (0, core * half), (width, half))
    early = product_left_t(jnp.where(is_lower, odd3[1], odd3[2]), own_h)
    early, recv_h = lax.optimization_barrier((early, recv_h))
    update = early + product_left_t(jnp.where(is_lower, odd3[2], odd3[1]), recv_h)
    upper_h = jnp.where(is_lower, recv_h, own_h)
    level0_out = upper_h - product(odd3[0], update)
    chain = jnp.where(is_lower, own_h, recv_h) - update

    zeros = jnp.zeros_like(tree_factor)
    result = chain
    for level in range(1, levels):
        step = 1 << level
        phase = base % (2 * step)
        is_lower = phase == 0
        is_upper = phase == step
        pairs = []
        for i in range(0, n_row, 2 * step):
            for c in range(2):
                pairs += [(i + c, i + step + c), (i + step + c, i + c)]
        q = product_left_t(jnp.where(is_upper, even3[2], zeros), chain)
        received = lax.ppermute(jnp.where(is_upper, q, chain), "row", pairs)
        mine = partner_factors[level - 1]
        mates = lax.ppermute(mine, "row", swap)
        top_rows = jnp.where(is_lower & (core == 0), mine, jnp.where(is_lower, mates, 0.0))
        bottom_rows = jnp.where(is_lower & (core == 0), mates, jnp.where(is_lower, mine, 0.0))
        own_part = product_left_t(top_rows, chain[:hw]) + product_left_t(bottom_rows, chain[hw:])
        own_part, received = lax.optimization_barrier((own_part, received))
        update = product_left_t(even3[1], received) + q
        result = jnp.where(is_upper, chain - product(even3[0], update), result)
        chain = jnp.where(is_lower, chain - own_part - received, chain)
    base_out = jnp.where(base == 0, chain, result)

    keep = jnp.where(core == 0, base_out, level0_out)
    give = jnp.where(core == 0, level0_out, base_out)
    got = lax.ppermute(give, "row", swap)
    top = jnp.concatenate([jnp.where(core == 0, keep, got), jnp.where(core == 0, got, keep)], axis=1)
    return jnp.concatenate([top, remainder], axis=0)


def solution(mesh):
    in_specs = (P("row", "col"), P("row", "col"), P("row", "col"), P("row", "col"), P("row", "col"))
    out_specs = P("row", "col")
    return jax.shard_map(
        on_device, mesh=mesh, in_specs=in_specs, out_specs=out_specs, check_vma=False
    )
```
